256 devices in a mesh: lon: 32 (over z, x_hi, core), lat: 8 (over y, x_lo).
Axes of the slice: x: 4 (x_hi: 2, x_lo: 2; x = x_hi * 2 + x_lo), y: 4, z: 8, core: 2. Of those that a mesh axis runs over, the one named last changes fastest.
Arguments:
- inputs: bfloat16 [384, 1536, 128], P('lat', 'lon'), may hold values from -6 to 6
- weight: bfloat16 [3, 3, 128, 128], replicated, may hold values from -0.1875 to 0.1875
- bias: float32 [128], replicated, may hold values from -3 to 3
- cotangent: bfloat16 [384, 1536, 128], P('lat', 'lon'), may hold values from -6 to 6
Outputs:
- outputs: bfloat16 [384, 1536, 128], P('lat', 'lon')
- input_grad: bfloat16 [384, 1536, 128], P('lat', 'lon')
- weight_grad: float32 [3, 3, 128, 128], replicated
- bias_grad: float32 [128], replicated
The draws below stay inside these ranges and needn't reach their ends.
All inputs are finite; a program needn't handle non-finite values.
Results may differ from the reference program's by a relative error of at most 0.006.
Values may be sent and summed in bfloat16 or wider, within the bound.
No kernel may reach another device: no remote copies, remote signals or barrier semaphores. Data moves between devices by JAX's collectives and lax.ppermute only.
A program may use at most 64 MiB of HBM per device.

```python
import jax
import jax.numpy as jnp
from jax import lax

C = 128
NLAT = 384
NLON = 1536


def block_scale(rng, shape, split, low, high):
    def one(axis_at, parts):
        draws = jax.random.uniform(jax.random.fold_in(jax.random.fold_in(rng, 6), axis_at), (parts,), jnp.float32, low / len(split), high / len(split))
        return jnp.repeat(jnp.exp(draws), shape[axis_at] // parts).reshape((-1,) + (1,) * (len(shape) - axis_at - 1))

    level = one(*split[0])
    for cut in split[1:]:
        level = level * one(*cut)
    return level


def normal_values(stream_key, extent, deviation, most, cuts=(), kind=jnp.bfloat16):
    gain = block_scale(stream_key, extent, cuts, -0.22, 0.18) if cuts else 1.0
    entries = jax.random.normal(stream_key, extent, jnp.float32) * deviation * gain
    return jnp.minimum(jnp.maximum(entries, -most), most).astype(kind)


def setup_inputs(seed: int = 0) -> dict:
    arg_keys = jax.random.split(jax.random.key(seed), 5)
    inputs = normal_values(arg_keys[0], (NLAT, NLON, C), 1.0, 6.0, ((0, 8), (1, 32)))
    weight = normal_values(arg_keys[1], (3, 3, C, C), (9 * C) ** -0.5, 0.1875)
    bias = normal_values(arg_keys[2], (C,), 0.5, 3.0, (), jnp.float32)
    cotangent = normal_values(arg_keys[3], (NLAT, NLON, C), 1.0, 6.0, ((0, 8), (1, 32)))
    return dict(inputs=inputs, weight=weight, bias=bias, cotangent=cotangent)


def pad_field(field):
    half = field.shape[1] // 2
    wide = jnp.concatenate([field[:, -1:], field, field[:, :1]], axis=1)
    top = jnp.roll(field[0], -half, axis=0)
    bottom = jnp.roll(field[-1], -half, axis=0)
    top_wide = jnp.concatenate([top[-1:], top, top[:1]], axis=0)
    bottom_wide = jnp.concatenate([bottom[-1:], bottom, bottom[:1]], axis=0)
    return jnp.concatenate([top_wide[None], wide, bottom_wide[None]], axis=0)

def reference(inputs, weight, bias, cotangent):
    rows, cols, chans = inputs.shape
    padded = pad_field(inputs)
    pre = jnp.zeros((rows * cols, chans), jnp.float32) + bias[None, :]
    for tap_a in range(3):
        for tap_b in range(3):
            window = padded[tap_a:tap_a + rows, tap_b:tap_b + cols].reshape(rows * cols, chans)
            pre = pre + jnp.dot(window, weight[tap_a, tap_b], preferred_element_type=jnp.float32)
    sig = jax.nn.sigmoid(pre)
    outputs = (pre * sig).astype(jnp.bfloat16).reshape(rows, cols, chans)
    flat_cot = cotangent.reshape(rows * cols, chans).astype(jnp.float32)
    pre_grad = (flat_cot * sig * (1.0 + pre * (1.0 - sig))).astype(jnp.bfloat16)
    padded_grad = jnp.zeros((rows + 2, cols + 2, chans), jnp.float32)
    scale = 1.0 / jnp.sqrt(jnp.float32(rows * cols))
    taps = []
    for tap_a in range(3):
        for tap_b in range(3):
            back = jnp.dot(pre_grad, weight[tap_a, tap_b].T, preferred_element_type=jnp.float32)
            padded_grad = padded_grad.at[tap_a:tap_a + rows, tap_b:tap_b + cols].add(back.reshape(rows, cols, chans))
            window = padded[tap_a:tap_a + rows, tap_b:tap_b + cols].reshape(rows * cols, chans)
            taps.append(lax.dot_general(window, pre_grad, (((0,), (0,)), ((), ())), preferred_element_type=jnp.float32))
    weight_grad = jnp.stack(taps).reshape(3, 3, chans, chans) * scale
    bias_grad = lax.optimization_barrier(jnp.sum(pre_grad.astype(jnp.float32), axis=0)) * scale
    unused, pull = jax.vjp(pad_field, inputs.astype(jnp.float32))
    input_grad = pull(padded_grad)[0].astype(jnp.bfloat16)
    return (outputs, input_grad, weight_grad, bias_grad)
```

```python
import jax
import jax.numpy as jnp
from jax import lax
from jax.sharding import PartitionSpec as P


def extended(cells, sides, width, closed):
    for axis, dim in sides:
        count = lax.axis_size(axis)
        ends = count if closed else count - 1
        head = lax.slice_in_dim(cells, 0, width, axis=dim)
        tail = lax.slice_in_dim(cells, cells.shape[dim] - width, cells.shape[dim], axis=dim)
        cells = jnp.concatenate(
            [
                lax.ppermute(tail, axis, [(i, (i + 1) % count) for i in range(ends)]),
                cells,
                lax.ppermute(head, axis, [((i + 1) % count, i) for i in range(ends)]),
            ],
            axis=dim,
        )
    return cells


def from_behind(value, axis, steps):
    count = lax.axis_size(axis)
    pairs = [(source, (source + steps) % count) for source in range(count)]
    return lax.ppermute(value, axis, pairs)


def butterfly_sum(value, order):
    shape = value.shape
    data = value.reshape(-1)
    parts = 1
    for axis, _ in order:
        parts *= 2
    pad = (-data.shape[0]) % parts
    data = jnp.pad(data, (0, pad))
    history = []
    for axis, step in order:
        count = lax.axis_size(axis)
        bit = (lax.axis_index(axis) // step) % 2
        half = data.shape[0] // 2
        pairs = [(i, i ^ step) for i in range(count)]
        send = lax.dynamic_slice_in_dim(data, (1 - bit) * half, half)
        keep = lax.dynamic_slice_in_dim(data, bit * half, half)
        data = keep + lax.ppermute(send, axis, pairs)
        history.append((axis, step, bit))
    for axis, step, bit in reversed(history):
        count = lax.axis_size(axis)
        pairs = [(i, i ^ step) for i in range(count)]
        other = lax.ppermute(data, axis, pairs)
        data = jnp.where(bit == 0, jnp.concatenate([data, other]), jnp.concatenate([other, data]))
    return data[: data.shape[0] - pad].reshape(shape)


def halving_order(mesh_axes):
    order = []
    steps = {axis: 1 for axis in mesh_axes}
    while any(steps[axis] < lax.axis_size(axis) for axis in mesh_axes):
        for axis in mesh_axes:
            if steps[axis] < lax.axis_size(axis):
                order.append((axis, steps[axis]))
                steps[axis] *= 2
    return order


def shards(inputs, weight, bias, cotangent):
    rows, cols, chans = inputs.shape
    band = lax.axis_index("lat")
    bands = lax.axis_size("lat")
    half = lax.axis_size("lon") // 2
    wide = extended(inputs, (("lon", 1),), 1, True)
    tall = extended(wide, (("lat", 0),), 1, False)
    far_top, far_bottom = from_behind((wide[0], wide[-1]), "lon", half)
    top = jnp.where(band == 0, far_top, tall[0])
    bottom = jnp.where(band == bands - 1, far_bottom, tall[-1])
    padded = jnp.concatenate([top[None], tall[1:-1], bottom[None]], axis=0)
    pre = jnp.zeros((rows * cols, chans), jnp.float32) + bias[None, :]
    for tap_a in range(3):
        for tap_b in range(3):
            window = padded[tap_a : tap_a + rows, tap_b : tap_b + cols].reshape(rows * cols, chans)
            pre = pre + jnp.dot(window, weight[tap_a, tap_b], preferred_element_type=jnp.float32)
    sig = jax.nn.sigmoid(pre)
    outputs = (pre * sig).astype(jnp.bfloat16).reshape(rows, cols, chans)
    flat_cot = cotangent.reshape(rows * cols, chans).astype(jnp.float32)
    pre_grad = (flat_cot * sig * (1.0 + pre * (1.0 - sig))).astype(jnp.bfloat16)
    grad_cells = pre_grad.reshape(rows, cols, chans)
    flipped = jnp.transpose(weight[::-1, ::-1], (0, 1, 3, 2))
    padded_grad = lax.conv_general_dilated(
        jnp.pad(grad_cells, ((2, 2), (2, 2), (0, 0)))[None],
        flipped,
        (1, 1),
        "VALID",
        dimension_numbers=("NHWC", "HWIO", "NHWC"),
        preferred_element_type=jnp.float32,
    )[0]
    taps = []
    for tap_a in range(3):
        for tap_b in range(3):
            window = padded[tap_a : tap_a + rows, tap_b : tap_b + cols].reshape(rows * cols, chans)
            taps.append(
                lax.dot_general(
                    window, pre_grad, (((0,), (0,)), ((), ())), preferred_element_type=jnp.float32
                )
            )
    kernel_terms = jnp.concatenate(taps, axis=0)
    bias_terms = jnp.sum(pre_grad.astype(jnp.float32), axis=0)[None, :]
    edges = jnp.stack([padded_grad[0], padded_grad[-1]], axis=0)
    beside_all = extended(edges.astype(jnp.bfloat16), (("lat", 0),), 1, False).astype(edges.dtype)
    polar_top, polar_bottom = (
        from_behind(padded_grad[0].astype(jnp.bfloat16), "lon", half).astype(jnp.float32),
        from_behind(padded_grad[-1].astype(jnp.bfloat16), "lon", half).astype(jnp.float32),
    )
    inner = padded_grad[1:-1]
    inner = inner.at[0].add(beside_all[0] + jnp.where(band == 0, polar_top, 0.0))
    inner = inner.at[-1].add(beside_all[3] + jnp.where(band == bands - 1, polar_bottom, 0.0))
    sides = jnp.stack([inner[:, 0], inner[:, -1]], axis=1)
    beside = extended(sides.astype(jnp.bfloat16), (("lon", 1),), 1, True).astype(sides.dtype)
    core = inner[:, 1:-1]
    core = core.at[:, 0].add(beside[:, 0])
    core = core.at[:, -1].add(beside[:, 3])
    input_grad = core.astype(jnp.bfloat16)
    sums = butterfly_sum(jnp.concatenate([kernel_terms, bias_terms], axis=0), halving_order(("lon", "lat")))
    kernel_sum, bias_sum = sums[:-1], sums[-1:]
    total_cells = rows * cols * lax.axis_size("lon") * lax.axis_size("lat")
    scale = 1.0 / jnp.sqrt(jnp.float32(total_cells))
    weight_grad = kernel_sum.reshape(3, 3, chans, chans) * scale
    bias_grad = bias_sum[0] * scale
    return (outputs, input_grad, weight_grad, bias_grad)


def solution(mesh):
    in_specs = (P("lat", "lon", None), P(), P(), P("lat", "lon", None))
    out_specs = (P("lat", "lon", None), P("lat", "lon", None), P(), P())
    return jax.shard_map(shards, mesh=mesh, in_specs=in_specs, out_specs=out_specs, check_vma=False)
```

```python
import jax
import jax.numpy as jnp
from jax import lax
from jax.sharding import PartitionSpec as P


def extended(cells, sides, width, closed):
    for axis, dim in sides:
        count = lax.axis_size(axis)
        ends = count if closed else count - 1
        head = lax.slice_in_dim(cells, 0, width, axis=dim)
        tail = lax.slice_in_dim(cells, cells.shape[dim] - width, cells.shape[dim], axis=dim)
        cells = jnp.concatenate(
            [
                lax.ppermute(tail, axis, [(i, (i + 1) % count) for i in range(ends)]),
                cells,
                lax.ppermute(head, axis, [((i + 1) % count, i) for i in range(ends)]),
            ],
            axis=dim,
        )
    return cells


def from_behind(value, axis, steps):
    count = lax.axis_size(axis)
    pairs = [(source, (source + steps) % count) for source in range(count)]
    return lax.ppermute(value, axis, pairs)


def butterfly_sum(value, scatter, double):
    shape = value.shape
    data = value.reshape(-1)
    parts = 2 ** len(scatter)
    pad = (-data.shape[0]) % parts
    data = jnp.pad(data, (0, pad))
    history = []
    for axis, step in scatter:
        count = lax.axis_size(axis)
        bit = (lax.axis_index(axis) // step) % 2
        half = data.shape[0] // 2
        pairs = [(i, i ^ step) for i in range(count)]
        send = lax.dynamic_slice_in_dim(data, (1 - bit) * half, half)
        keep = lax.dynamic_slice_in_dim(data, bit * half, half)
        data = keep + lax.ppermute(send, axis, pairs)
        history.append((axis, step, bit))
    for axis, step in double:
        count = lax.axis_size(axis)
        pairs = [(i, i ^ step) for i in range(count)]
        data = data + lax.ppermute(data, axis, pairs)
    for axis, step, bit in reversed(history):
        count = lax.axis_size(axis)
        pairs = [(i, i ^ step) for i in range(count)]
        other = lax.ppermute(data, axis, pairs)
        data = jnp.where(bit == 0, jnp.concatenate([data, other]), jnp.concatenate([other, data]))
    return data[: data.shape[0] - pad].reshape(shape)


def pairing_order(mesh_axes):
    near = []
    for axis in mesh_axes:
        step = 1
        while step < lax.axis_size(axis):
            near.append((axis, step))
            step *= 2
    ranked = [("lon", 1), ("lat", 1), ("lon", 4), ("lat", 2)]
    first = [pair for pair in ranked if pair in near]
    rest = [pair for pair in near if pair not in first]
    return first + rest


def shards(inputs, weight, bias, cotangent):
    rows, cols, chans = inputs.shape
    band = lax.axis_index("lat")
    bands = lax.axis_size("lat")
    half = lax.axis_size("lon") // 2
    wide = extended(inputs, (("lon", 1),), 1, True)
    tall = extended(wide, (("lat", 0),), 1, False)
    far_top, far_bottom = from_behind((wide[0], wide[-1]), "lon", half)
    top = jnp.where(band == 0, far_top, tall[0])
    bottom = jnp.where(band == bands - 1, far_bottom, tall[-1])
    padded = jnp.concatenate([top[None], tall[1:-1], bottom[None]], axis=0)
    pre = jnp.zeros((rows * cols, chans), jnp.float32) + bias[None, :]
    for tap_a in range(3):
        for tap_b in range(3):
            window = padded[tap_a : tap_a + rows, tap_b : tap_b + cols].reshape(rows * cols, chans)
            pre = pre + jnp.dot(window, weight[tap_a, tap_b], preferred_element_type=jnp.float32)
    sig = jax.nn.sigmoid(pre)
    outputs = (pre * sig).astype(jnp.bfloat16).reshape(rows, cols, chans)
    flat_cot = cotangent.reshape(rows * cols, chans).astype(jnp.float32)
    pre_grad = (flat_cot * sig * (1.0 + pre * (1.0 - sig))).astype(jnp.bfloat16)
    grad_cells = pre_grad.reshape(rows, cols, chans)
    flipped = jnp.transpose(weight[::-1, ::-1], (0, 1, 3, 2))
    padded_grad = lax.conv_general_dilated(
        jnp.pad(grad_cells, ((2, 2), (2, 2), (0, 0)))[None],
        flipped,
        (1, 1),
        "VALID",
        dimension_numbers=("NHWC", "HWIO", "NHWC"),
        preferred_element_type=jnp.float32,
    )[0]
    taps = []
    for tap_a in range(3):
        for tap_b in range(3):
            window = padded[tap_a : tap_a + rows, tap_b : tap_b + cols].reshape(rows * cols, chans)
            taps.append(
                lax.dot_general(
                    window, pre_grad, (((0,), (0,)), ((), ())), preferred_element_type=jnp.float32
                )
            )
    kernel_terms = jnp.concatenate(taps, axis=0)
    bias_terms = jnp.sum(pre_grad.astype(jnp.float32), axis=0)[None, :]
    edges = jnp.stack([padded_grad[0], padded_grad[-1]], axis=0)
    beside_all = extended(edges.astype(jnp.bfloat16), (("lat", 0),), 1, False).astype(edges.dtype)
    polar_top, polar_bottom = (
        from_behind(padded_grad[0].astype(jnp.bfloat16), "lon", half).astype(jnp.float32),
        from_behind(padded_grad[-1].astype(jnp.bfloat16), "lon", half).astype(jnp.float32),
    )
    inner = padded_grad[1:-1]
    inner = inner.at[0].add(beside_all[0] + jnp.where(band == 0, polar_top, 0.0))
    inner = inner.at[-1].add(beside_all[3] + jnp.where(band == bands - 1, polar_bottom, 0.0))
    sides = jnp.stack([inner[:, 0], inner[:, -1]], axis=1)
    beside = extended(sides.astype(jnp.bfloat16), (("lon", 1),), 1, True).astype(sides.dtype)
    core = inner[:, 1:-1]
    core = core.at[:, 0].add(beside[:, 0])
    core = core.at[:, -1].add(beside[:, 3])
    input_grad = core.astype(jnp.bfloat16)
    order = pairing_order(("lon", "lat"))
    sums = butterfly_sum(jnp.concatenate([kernel_terms, bias_terms], axis=0), order[:3], order[3:])
    kernel_sum, bias_sum = sums[:-1], sums[-1:]
    total_cells = rows * cols * lax.axis_size("lon") * lax.axis_size("lat")
    scale = 1.0 / jnp.sqrt(jnp.float32(total_cells))
    weight_grad = kernel_sum.reshape(3, 3, chans, chans) * scale
    bias_grad = bias_sum[0] * scale
    return (outputs, input_grad, weight_grad, bias_grad)


def solution(mesh):
    in_specs = (P("lat", "lon", None), P(), P(), P("lat", "lon", None))
    out_specs = (P("lat", "lon", None), P("lat", "lon", None), P(), P())
    return jax.shard_map(shards, mesh=mesh, in_specs=in_specs, out_specs=out_specs, check_vma=False)
```

```python
import jax
import jax.numpy as jnp
from jax import lax
from jax.sharding import PartitionSpec as P


def extended(cells, sides, width, closed):
    for axis, dim in sides:
        count = lax.axis_size(axis)
        ends = count if closed else count - 1
        head = lax.slice_in_dim(cells, 0, width, axis=dim)
        tail = lax.slice_in_dim(cells, cells.shape[dim] - width, cells.shape[dim], axis=dim)
        cells = jnp.concatenate(
            [
                lax.ppermute(tail, axis, [(i, (i + 1) % count) for i in range(ends)]),
                cells,
                lax.ppermute(head, axis, [((i + 1) % count, i) for i in range(ends)]),
            ],
            axis=dim,
        )
    return cells


def from_behind(value, axis, steps):
    count = lax.axis_size(axis)
    pairs = [(source, (source + steps) % count) for source in range(count)]
    return lax.ppermute(value, axis, pairs)


def butterfly_sum(value, scatter, double):
    shape = value.shape
    data = value.reshape(-1)
    parts = 2 ** len(scatter)
    pad = (-data.shape[0]) % parts
    data = jnp.pad(data, (0, pad))
    history = []
    for axis, step in scatter:
        count = lax.axis_size(axis)
        bit = (lax.axis_index(axis) // step) % 2
        half = data.shape[0] // 2
        pairs = [(i, i ^ step) for i in range(count)]
        send = lax.dynamic_slice_in_dim(data, (1 - bit) * half, half)
        keep = lax.dynamic_slice_in_dim(data, bit * half, half)
        data = keep + lax.ppermute(send, axis, pairs)
        history.append((axis, step, bit))
    for axis, step in double:
        count = lax.axis_size(axis)
        pairs = [(i, i ^ step) for i in range(count)]
        data = data + lax.ppermute(data, axis, pairs)
    for axis, step, bit in reversed(history):
        count = lax.axis_size(axis)
        pairs = [(i, i ^ step) for i in range(count)]
        other = lax.ppermute(data, axis, pairs)
        data = jnp.where(bit == 0, jnp.concatenate([data, other]), jnp.concatenate([other, data]))
    return data[: data.shape[0] - pad].reshape(shape)


def pairing_order(mesh_axes):
    near = []
    for axis in mesh_axes:
        step = 1
        while step < lax.axis_size(axis):
            near.append((axis, step))
            step *= 2
    ranked = [("lon", 1), ("lat", 1), ("lon", 4), ("lat", 2)]
    first = [pair for pair in ranked if pair in near]
    rest = [pair for pair in near if pair not in first]
    return first + rest


def shards(inputs, weight, bias, cotangent):
    rows, cols, chans = inputs.shape
    band = lax.axis_index("lat")
    bands = lax.axis_size("lat")
    half = lax.axis_size("lon") // 2
    both = jnp.concatenate([inputs, cotangent], axis=2)
    wide = extended(both, (("lon", 1),), 2, True)
    tall = extended(wide, (("lat", 0),), 2, False)
    far = from_behind(jnp.stack([wide[0], wide[-1]]), "lon", half)
    tall = tall.at[1].set(jnp.where(band == 0, far[0], tall[1]))
    tall = tall.at[rows + 2].set(jnp.where(band == bands - 1, far[1], tall[rows + 2]))
    padded = tall[:, :, :chans]
    flat_cot = tall[1:-1, 1:-1, chans:].reshape((rows + 2) * (cols + 2), chans).astype(jnp.float32)
    pre = lax.conv_general_dilated(
        padded[None],
        weight,
        (1, 1),
        "VALID",
        dimension_numbers=("NHWC", "HWIO", "NHWC"),
        preferred_element_type=jnp.float32,
    )[0].reshape((rows + 2) * (cols + 2), chans) + bias[None, :]
    sig = jax.nn.sigmoid(pre)
    silu = (pre * sig).reshape(rows + 2, cols + 2, chans)
    outputs = silu[1:-1, 1:-1].astype(jnp.bfloat16)
    grad_ext = (flat_cot * sig * (1.0 + pre * (1.0 - sig))).astype(jnp.bfloat16).reshape(rows + 2, cols + 2, chans)
    line = lax.broadcasted_iota(jnp.int32, (rows + 2, 1, 1), 0)
    outside = ((line == 0) & (band == 0)) | ((line == rows + 1) & (band == bands - 1))
    grad_ext = jnp.where(outside, jnp.zeros_like(grad_ext), grad_ext)
    pre_grad = grad_ext[1:-1, 1:-1].reshape(rows * cols, chans)
    flipped = jnp.transpose(weight[::-1, ::-1], (0, 1, 3, 2))
    cell_grad = lax.conv_general_dilated(
        grad_ext[None],
        flipped,
        (1, 1),
        "VALID",
        dimension_numbers=("NHWC", "HWIO", "NHWC"),
        preferred_element_type=jnp.float32,
    )[0]
    polar = []
    for line_at, tap_a in ((1, 0), (rows, 2)):
        ring = jnp.zeros((cols, chans), jnp.float32)
        for tap_b in range(3):
            ring = ring + jnp.dot(
                grad_ext[line_at, tap_b : tap_b + cols],
                weight[tap_a, 2 - tap_b].T,
                preferred_element_type=jnp.float32,
            )
        polar.append(ring)
    polar_in = from_behind(jnp.stack(polar).astype(jnp.bfloat16), "lon", half).astype(jnp.float32)
    cell_grad = cell_grad.at[0].add(jnp.where(band == 0, polar_in[0], 0.0))
    cell_grad = cell_grad.at[-1].add(jnp.where(band == bands - 1, polar_in[1], 0.0))
    input_grad = cell_grad.astype(jnp.bfloat16)
    taps = []
    for tap_a in range(3):
        for tap_b in range(3):
            window = padded[tap_a + 1 : tap_a + 1 + rows, tap_b + 1 : tap_b + 1 + cols].reshape(rows * cols, chans)
            taps.append(
                lax.dot_general(
                    window, pre_grad, (((0,), (0,)), ((), ())), preferred_element_type=jnp.float32
                )
            )
    kernel_terms = jnp.concatenate(taps, axis=0)
    bias_terms = jnp.sum(pre_grad.astype(jnp.float32), axis=0)[None, :]
    order = pairing_order(("lon", "lat"))
    sums = butterfly_sum(jnp.concatenate([kernel_terms, bias_terms], axis=0), order[:3], order[3:])
    kernel_sum, bias_sum = sums[:-1], sums[-1:]
    total_cells = rows * cols * lax.axis_size("lon") * lax.axis_size("lat")
    scale = 1.0 / jnp.sqrt(jnp.float32(total_cells))
    weight_grad = kernel_sum.reshape(3, 3, chans, chans) * scale
    bias_grad = bias_sum[0] * scale
    return (outputs, input_grad, weight_grad, bias_grad)


def solution(mesh):
    in_specs = (P("lat", "lon", None), P(), P(), P("lat", "lon", None))
    out_specs = (P("lat", "lon", None), P("lat", "lon", None), P(), P())
    return jax.shard_map(shards, mesh=mesh, in_specs=in_specs, out_specs=out_specs, check_vma=False)
```

```python
import jax
import jax.numpy as jnp
from jax import lax
from jax.sharding import PartitionSpec as P


def extended(cells, sides, width, closed):
    for axis, dim in sides:
        count = lax.axis_size(axis)
        ends = count if closed else count - 1
        head = lax.slice_in_dim(cells, 0, width, axis=dim)
        tail = lax.slice_in_dim(cells, cells.shape[dim] - width, cells.shape[dim], axis=dim)
        cells = jnp.concatenate(
            [
                lax.ppermute(tail, axis, [(i, (i + 1) % count) for i in range(ends)]),
                cells,
                lax.ppermute(head, axis, [((i + 1) % count, i) for i in range(ends)]),
            ],
            axis=dim,
        )
    return cells


def from_behind(value, axis, steps):
    count = lax.axis_size(axis)
    pairs = [(source, (source + steps) % count) for source in range(count)]
    return lax.ppermute(value, axis, pairs)


def butterfly_sum(value, scatter, double):
    shape = value.shape
    data = value.reshape(-1)
    parts = 2 ** len(scatter)
    pad = (-data.shape[0]) % parts
    data = jnp.pad(data, (0, pad))
    history = []
    for axis, step in scatter:
        count = lax.axis_size(axis)
        bit = (lax.axis_index(axis) // step) % 2
        half = data.shape[0] // 2
        pairs = [(i, i ^ step) for i in range(count)]
        send = lax.dynamic_slice_in_dim(data, (1 - bit) * half, half)
        keep = lax.dynamic_slice_in_dim(data, bit * half, half)
        data = keep + lax.ppermute(send, axis, pairs)
        history.append((axis, step, bit))
    for axis, pairs in double:
        data = data + lax.ppermute(data, axis, pairs)
    for axis, step, bit in reversed(history):
        count = lax.axis_size(axis)
        pairs = [(i, i ^ step) for i in range(count)]
        other = lax.ppermute(data, axis, pairs)
        data = jnp.where(bit == 0, jnp.concatenate([data, other]), jnp.concatenate([other, data]))
    return data[: data.shape[0] - pad].reshape(shape)


def pairing_order(mesh_axes):
    near = []
    for axis in mesh_axes:
        step = 1
        while step < lax.axis_size(axis):
            near.append((axis, step))
            step *= 2
    ranked = [("lon", 1), ("lat", 1), ("lon", 4), ("lat", 2)]
    first = [pair for pair in ranked if pair in near]
    rest = [pair for pair in near if pair not in first]
    return first + rest


def reflected_ring_pairs(count, stride, size):
    pairs = []
    for i in range(count):
        z = (i // stride) % size
        if z % 2 == 0:
            w = (size - 2 - z) % size
        else:
            w = (size - z) % size
        pairs.append((i, i + (w - z) * stride))
    return pairs


def doubling_plan(rest):
    plan = []
    lon = lax.axis_size("lon")
    for axis, step in rest:
        count = lax.axis_size(axis)
        pairs = [(i, i ^ step) for i in range(count)]
        if axis == "lat" and step == 4 and count == 8:
            pairs = [(i, (3 - i // 2) * 2 + i % 2) for i in range(count)]
        if axis == "lon" and step == 16 and count == 32:
            pairs = reflected_ring_pairs(lon, 4, 8)
        plan.append((axis, pairs))
    return plan


def shards(inputs, weight, bias, cotangent):
    rows, cols, chans = inputs.shape
    band = lax.axis_index("lat")
    bands = lax.axis_size("lat")
    half = lax.axis_size("lon") // 2
    both = jnp.concatenate([inputs, cotangent], axis=2)
    wide = extended(both, (("lon", 1),), 2, True)
    tall = extended(wide, (("lat", 0),), 2, False)
    far = from_behind(jnp.stack([wide[0], wide[-1]]), "lon", half)
    tall = tall.at[1].set(jnp.where(band == 0, far[0], tall[1]))
    tall = tall.at[rows + 2].set(jnp.where(band == bands - 1, far[1], tall[rows + 2]))
    padded = tall[:, :, :chans]
    ring_cot = tall[1:-1, 1:-1, chans:].astype(jnp.float32)
    pre = lax.conv_general_dilated(
        padded[None],
        weight,
        (1, 1),
        "VALID",
        dimension_numbers=("NHWC", "HWIO", "NHWC"),
        preferred_element_type=jnp.float32,
    )[0] + bias
    sig = jax.nn.sigmoid(pre)
    outputs = (pre * sig)[1:-1, 1:-1].astype(jnp.bfloat16)
    grad_ext = (ring_cot * sig * (1.0 + pre * (1.0 - sig))).astype(jnp.bfloat16)
    line = lax.broadcasted_iota(jnp.int32, (rows + 2, 1, 1), 0)
    outside = ((line == 0) & (band == 0)) | ((line == rows + 1) & (band == bands - 1))
    grad_ext = jnp.where(outside, jnp.zeros_like(grad_ext), grad_ext)
    pre_grad = grad_ext[1:-1, 1:-1].reshape(rows * cols, chans)
    flipped = jnp.transpose(weight[::-1, ::-1], (0, 1, 3, 2))
    cell_grad = lax.conv_general_dilated(
        grad_ext[None],
        flipped,
        (1, 1),
        "VALID",
        dimension_numbers=("NHWC", "HWIO", "NHWC"),
        preferred_element_type=jnp.float32,
    )[0]
    polar = []
    for line_at, tap_a in ((1, 0), (rows, 2)):
        ring = jnp.zeros((cols, chans), jnp.float32)
        for tap_b in range(3):
            ring = ring + jnp.dot(
                grad_ext[line_at, tap_b : tap_b + cols],
                weight[tap_a, 2 - tap_b].T,
                preferred_element_type=jnp.float32,
            )
        polar.append(ring)
    polar_in = from_behind(jnp.stack(polar).astype(jnp.bfloat16), "lon", half).astype(jnp.float32)
    cell_grad = cell_grad.at[0].add(jnp.where(band == 0, polar_in[0], 0.0))
    cell_grad = cell_grad.at[-1].add(jnp.where(band == bands - 1, polar_in[1], 0.0))
    input_grad = cell_grad.astype(jnp.bfloat16)
    taps = []
    for tap_a in range(3):
        for tap_b in range(3):
            window = padded[tap_a + 1 : tap_a + 1 + rows, tap_b + 1 : tap_b + 1 + cols].reshape(rows * cols, chans)
            taps.append(
                lax.dot_general(
                    window, pre_grad, (((0,), (0,)), ((), ())), preferred_element_type=jnp.float32
                )
            )
    kernel_terms = jnp.concatenate(taps, axis=0)
    bias_terms = jnp.sum(pre_grad.astype(jnp.float32), axis=0)[None, :]
    order = pairing_order(("lon", "lat"))
    sums = butterfly_sum(jnp.concatenate([kernel_terms, bias_terms], axis=0), order[:3], doubling_plan(order[3:]))
    kernel_sum, bias_sum = sums[:-1], sums[-1:]
    total_cells = rows * cols * lax.axis_size("lon") * lax.axis_size("lat")
    scale = 1.0 / jnp.sqrt(jnp.float32(total_cells))
    weight_grad = kernel_sum.reshape(3, 3, chans, chans) * scale
    bias_grad = bias_sum[0] * scale
    return (outputs, input_grad, weight_grad, bias_grad)


def solution(mesh):
    in_specs = (P("lat", "lon", None), P(), P(), P("lat", "lon", None))
    out_specs = (P("lat", "lon", None), P("lat", "lon", None), P(), P())
    return jax.shard_map(shards, mesh=mesh, in_specs=in_specs, out_specs=out_specs, check_vma=False)
```

```python
import jax
import jax.numpy as jnp
from jax import lax
from jax.sharding import PartitionSpec as P


def extended(cells, sides, width, closed):
    for axis, dim in sides:
        count = lax.axis_size(axis)
        ends = count if closed else count - 1
        head = lax.slice_in_dim(cells, 0, width, axis=dim)
        tail = lax.slice_in_dim(cells, cells.shape[dim] - width, cells.shape[dim], axis=dim)
        cells = jnp.concatenate(
            [
                lax.ppermute(tail, axis, [(i, (i + 1) % count) for i in range(ends)]),
                cells,
                lax.ppermute(head, axis, [((i + 1) % count, i) for i in range(ends)]),
            ],
            axis=dim,
        )
    return cells


def from_behind(value, axis, steps):
    count = lax.axis_size(axis)
    pairs = [(source, (source + steps) % count) for source in range(count)]
    return lax.ppermute(value, axis, pairs)


def butterfly_sum(value, scatter, double):
    shape = value.shape
    data = value.reshape(-1)
    parts = 2 ** len(scatter)
    pad = (-data.shape[0]) % parts
    data = jnp.pad(data, (0, pad))
    history = []
    for axis, step in scatter:
        count = lax.axis_size(axis)
        bit = (lax.axis_index(axis) // step) % 2
        half = data.shape[0] // 2
        pairs = [(i, i ^ step) for i in range(count)]
        send = lax.dynamic_slice_in_dim(data, (1 - bit) * half, half)
        keep = lax.dynamic_slice_in_dim(data, bit * half, half)
        data = keep + lax.ppermute(send, axis, pairs)
        history.append((axis, step, bit))
    for axis, pairs in double:
        data = data + lax.ppermute(data, axis, pairs)
    for axis, step, bit in reversed(history):
        count = lax.axis_size(axis)
        pairs = [(i, i ^ step) for i in range(count)]
        other = lax.ppermute(data, axis, pairs)
        data = jnp.where(bit == 0, jnp.concatenate([data, other]), jnp.concatenate([other, data]))
    return data[: data.shape[0] - pad].reshape(shape)


def pairing_order(mesh_axes):
    near = []
    for axis in mesh_axes:
        step = 1
        while step < lax.axis_size(axis):
            near.append((axis, step))
            step *= 2
    ranked = [("lon", 1), ("lat", 1), ("lon", 4), ("lat", 2)]
    first = [pair for pair in ranked if pair in near]
    rest = [pair for pair in near if pair not in first]
    return first + rest


def reflected_ring_pairs(count, stride, size):
    pairs = []
    for i in range(count):
        z = (i // stride) % size
        if z % 2 == 0:
            w = (size - 2 - z) % size
        else:
            w = (size - z) % size
        pairs.append((i, i + (w - z) * stride))
    return pairs


def doubling_plan(rest):
    plan = []
    lon = lax.axis_size("lon")
    for axis, step in rest:
        count = lax.axis_size(axis)
        pairs = [(i, i ^ step) for i in range(count)]
        if axis == "lat" and step == 4 and count == 8:
            pairs = [(i, (3 - i // 2) * 2 + i % 2) for i in range(count)]
        if axis == "lon" and step == 16 and count == 32:
            pairs = reflected_ring_pairs(lon, 4, 8)
        plan.append((axis, pairs))
    return plan


def shards(inputs, weight, bias, cotangent):
    rows, cols, chans = inputs.shape
    band = lax.axis_index("lat")
    bands = lax.axis_size("lat")
    half = lax.axis_size("lon") // 2
    both = jnp.concatenate([inputs, cotangent], axis=2)
    wide = extended(both, (("lon", 1),), 2, True)
    tall = extended(wide, (("lat", 0),), 2, False)
    far = from_behind(jnp.stack([wide[0], wide[1], wide[-2], wide[-1]]), "lon", half)
    tall = tall.at[1].set(jnp.where(band == 0, far[0], tall[1]))
    tall = tall.at[rows + 2].set(jnp.where(band == bands - 1, far[3], tall[rows + 2]))
    padded = tall[:, :, :chans]
    ring_cot = tall[1:-1, 1:-1, chans:].astype(jnp.float32)
    pre = lax.conv_general_dilated(
        padded[None],
        weight,
        (1, 1),
        "VALID",
        dimension_numbers=("NHWC", "HWIO", "NHWC"),
        preferred_element_type=jnp.float32,
    )[0] + bias
    sig = jax.nn.sigmoid(pre)
    outputs = (pre * sig)[1:-1, 1:-1].astype(jnp.bfloat16)
    grad_ext = (ring_cot * sig * (1.0 + pre * (1.0 - sig))).astype(jnp.bfloat16)
    line = lax.broadcasted_iota(jnp.int32, (rows + 2, 1, 1), 0)
    outside = ((line == 0) & (band == 0)) | ((line == rows + 1) & (band == bands - 1))
    grad_ext = jnp.where(outside, jnp.zeros_like(grad_ext), grad_ext)
    pre_grad = grad_ext[1:-1, 1:-1].reshape(rows * cols, chans)
    flipped = jnp.transpose(weight[::-1, ::-1], (0, 1, 3, 2))
    cell_grad = lax.conv_general_dilated(
        grad_ext[None],
        flipped,
        (1, 1),
        "VALID",
        dimension_numbers=("NHWC", "HWIO", "NHWC"),
        preferred_element_type=jnp.float32,
    )[0]
    polar = []
    for window, cot_line, tap_a in (
        (jnp.stack([wide[0], far[0], far[1]]), far[0], 0),
        (jnp.stack([far[2], far[3], wide[-1]]), far[3], 2),
    ):
        pre_line = lax.conv_general_dilated(
            window[None, :, :, :chans],
            weight,
            (1, 1),
            "VALID",
            dimension_numbers=("NHWC", "HWIO", "NHWC"),
            preferred_element_type=jnp.float32,
        )[0, 0] + bias
        sig_line = jax.nn.sigmoid(pre_line)
        cot_far = cot_line[1:-1, chans:].astype(jnp.float32)
        grad_line = (cot_far * sig_line * (1.0 + pre_line * (1.0 - sig_line))).astype(jnp.bfloat16)
        ring = jnp.zeros((cols, chans), jnp.float32)
        for tap_b in range(3):
            ring = ring + jnp.dot(
                grad_line[tap_b : tap_b + cols],
                weight[tap_a, 2 - tap_b].T,
                preferred_element_type=jnp.float32,
            )
        polar.append(ring)
    cell_grad = cell_grad.at[0].add(jnp.where(band == 0, polar[0], 0.0))
    cell_grad = cell_grad.at[-1].add(jnp.where(band == bands - 1, polar[1], 0.0))
    input_grad = cell_grad.astype(jnp.bfloat16)
    taps = []
    for tap_a in range(3):
        for tap_b in range(3):
            window = padded[tap_a + 1 : tap_a + 1 + rows, tap_b + 1 : tap_b + 1 + cols].reshape(rows * cols, chans)
            taps.append(
                lax.dot_general(
                    window, pre_grad, (((0,), (0,)), ((), ())), preferred_element_type=jnp.float32
                )
            )
    kernel_terms = jnp.concatenate(taps, axis=0)
    bias_terms = jnp.sum(pre_grad.astype(jnp.float32), axis=0)[None, :]
    order = pairing_order(("lon", "lat"))
    sums = butterfly_sum(jnp.concatenate([kernel_terms, bias_terms], axis=0), order[:3], doubling_plan(order[3:]))
    kernel_sum, bias_sum = sums[:-1], sums[-1:]
    total_cells = rows * cols * lax.axis_size("lon") * lax.axis_size("lat")
    scale = 1.0 / jnp.sqrt(jnp.float32(total_cells))
    weight_grad = kernel_sum.reshape(3, 3, chans, chans) * scale
    bias_grad = bias_sum[0] * scale
    return (outputs, input_grad, weight_grad, bias_grad)


def solution(mesh):
    in_specs = (P("lat", "lon", None), P(), P(), P("lat", "lon", None))
    out_specs = (P("lat", "lon", None), P("lat", "lon", None), P(), P())
    return jax.shard_map(shards, mesh=mesh, in_specs=in_specs, out_specs=out_specs, check_vma=False)
```

```python
import jax
import jax.numpy as jnp
from jax import lax
from jax.sharding import PartitionSpec as P


def extended(cells, sides, width, closed):
    for axis, dim in sides:
        count = lax.axis_size(axis)
        ends = count if closed else count - 1
        head = lax.slice_in_dim(cells, 0, width, axis=dim)
        tail = lax.slice_in_dim(cells, cells.shape[dim] - width, cells.shape[dim], axis=dim)
        cells = jnp.concatenate(
            [
                lax.ppermute(tail, axis, [(i, (i + 1) % count) for i in range(ends)]),
                cells,
                lax.ppermute(head, axis, [((i + 1) % count, i) for i in range(ends)]),
            ],
            axis=dim,
        )
    return cells


def from_behind(value, axis, steps):
    count = lax.axis_size(axis)
    pairs = [(source, (source + steps) % count) for source in range(count)]
    return lax.ppermute(value, axis, pairs)


def butterfly_sum(value, scatter, double):
    shape = value.shape
    data = value.reshape(-1)
    parts = 2 ** len(scatter)
    pad = (-data.shape[0]) % parts
    data = jnp.pad(data, (0, pad))
    history = []
    for axis, step in scatter:
        count = lax.axis_size(axis)
        bit = (lax.axis_index(axis) // step) % 2
        half = data.shape[0] // 2
        pairs = [(i, i ^ step) for i in range(count)]
        send = lax.dynamic_slice_in_dim(data, (1 - bit) * half, half)
        keep = lax.dynamic_slice_in_dim(data, bit * half, half)
        data = keep + lax.ppermute(send, axis, pairs)
        history.append((axis, step, bit))
    for axis, pairs in double:
        data = data + lax.ppermute(data, axis, pairs)
    for axis, step, bit in reversed(history):
        count = lax.axis_size(axis)
        pairs = [(i, i ^ step) for i in range(count)]
        other = lax.ppermute(data, axis, pairs)
        data = jnp.where(bit == 0, jnp.concatenate([data, other]), jnp.concatenate([other, data]))
    return data[: data.shape[0] - pad].reshape(shape)


def pairing_order(mesh_axes):
    near = []
    for axis in mesh_axes:
        step = 1
        while step < lax.axis_size(axis):
            near.append((axis, step))
            step *= 2
    ranked = [("lon", 1), ("lat", 1), ("lon", 4), ("lat", 2)]
    first = [pair for pair in ranked if pair in near]
    rest = [pair for pair in near if pair not in first]
    return first + rest


def reflected_ring_pairs(count, stride, size):
    pairs = []
    for i in range(count):
        z = (i // stride) % size
        if z % 2 == 0:
            w = (size - 2 - z) % size
        else:
            w = (size - z) % size
        pairs.append((i, i + (w - z) * stride))
    return pairs


def doubling_plan(rest):
    plan = []
    lon = lax.axis_size("lon")
    for axis, step in rest:
        count = lax.axis_size(axis)
        pairs = [(i, i ^ step) for i in range(count)]
        if axis == "lat" and step == 4 and count == 8:
            pairs = [(i, (3 - i // 2) * 2 + i % 2) for i in range(count)]
        if axis == "lon" and step == 16 and count == 32:
            pairs = reflected_ring_pairs(lon, 4, 8)
        plan.append((axis, pairs))
    return plan


def shards(inputs, weight, bias, cotangent):
    rows, cols, chans = inputs.shape
    band = lax.axis_index("lat")
    bands = lax.axis_size("lat")
    half = lax.axis_size("lon") // 2
    both = jnp.concatenate([inputs, cotangent], axis=2)
    wide = extended(both, (("lon", 1),), 2, True)
    tall = extended(wide, (("lat", 0),), 2, False)
    far = from_behind(jnp.stack([wide[0], wide[1], wide[-2], wide[-1]]), "lon", half)
    tall = tall.at[1].set(jnp.where(band == 0, far[0], tall[1]))
    tall = tall.at[rows + 2].set(jnp.where(band == bands - 1, far[3], tall[rows + 2]))
    padded = tall[:, :, :chans]
    ring_cot = tall[1:-1, 1:-1, chans:].astype(jnp.float32)
    pre = lax.conv_general_dilated(
        padded[None],
        weight,
        (1, 1),
        "VALID",
        dimension_numbers=("NHWC", "HWIO", "NHWC"),
        preferred_element_type=jnp.float32,
    )[0] + bias
    sig = jax.nn.sigmoid(pre)
    outputs = (pre * sig)[1:-1, 1:-1].astype(jnp.bfloat16)
    grad_ext = (ring_cot * sig * (1.0 + pre * (1.0 - sig))).astype(jnp.bfloat16)
    line = lax.broadcasted_iota(jnp.int32, (rows + 2, 1, 1), 0)
    outside = ((line == 0) & (band == 0)) | ((line == rows + 1) & (band == bands - 1))
    grad_ext = jnp.where(outside, jnp.zeros_like(grad_ext), grad_ext)
    pre_grad = grad_ext[1:-1, 1:-1].reshape(rows * cols, chans)
    flipped = jnp.transpose(weight[::-1, ::-1], (0, 1, 3, 2))
    cell_grad = lax.conv_general_dilated(
        grad_ext[None],
        flipped,
        (1, 1),
        "VALID",
        dimension_numbers=("NHWC", "HWIO", "NHWC"),
        preferred_element_type=jnp.float32,
    )[0]
    polar = []
    for window, cot_line, tap_a in (
        (jnp.stack([wide[0], far[0], far[1]]), far[0], 0),
        (jnp.stack([far[2], far[3], wide[-1]]), far[3], 2),
    ):
        pre_line = bias + jnp.zeros((cols + 2, chans), jnp.float32)
        for tap_a_in in range(3):
            for tap_b_in in range(3):
                pre_line = pre_line + jnp.dot(
                    window[tap_a_in, tap_b_in : tap_b_in + cols + 2, :chans],
                    weight[tap_a_in, tap_b_in],
                    preferred_element_type=jnp.float32,
                )
        sig_line = jax.nn.sigmoid(pre_line)
        cot_far = cot_line[1:-1, chans:].astype(jnp.float32)
        grad_line = (cot_far * sig_line * (1.0 + pre_line * (1.0 - sig_line))).astype(jnp.bfloat16)
        ring = jnp.zeros((cols, chans), jnp.float32)
        for tap_b in range(3):
            ring = ring + jnp.dot(
                grad_line[tap_b : tap_b + cols],
                weight[tap_a, 2 - tap_b].T,
                preferred_element_type=jnp.float32,
            )
        polar.append(ring)
    cell_grad = cell_grad.at[0].add(jnp.where(band == 0, polar[0], 0.0))
    cell_grad = cell_grad.at[-1].add(jnp.where(band == bands - 1, polar[1], 0.0))
    input_grad = cell_grad.astype(jnp.bfloat16)
    taps = []
    for tap_a in range(3):
        for tap_b in range(3):
            window = padded[tap_a + 1 : tap_a + 1 + rows, tap_b + 1 : tap_b + 1 + cols].reshape(rows * cols, chans)
            taps.append(
                lax.dot_general(
                    window, pre_grad, (((0,), (0,)), ((), ())), preferred_element_type=jnp.float32
                )
            )
    kernel_terms = jnp.concatenate(taps, axis=0)
    bias_terms = jnp.sum(pre_grad.astype(jnp.float32), axis=0)[None, :]
    order = pairing_order(("lon", "lat"))
    sums = butterfly_sum(jnp.concatenate([kernel_terms, bias_terms], axis=0), order[:3], doubling_plan(order[3:]))
    kernel_sum, bias_sum = sums[:-1], sums[-1:]
    total_cells = rows * cols * lax.axis_size("lon") * lax.axis_size("lat")
    scale = 1.0 / jnp.sqrt(jnp.float32(total_cells))
    weight_grad = kernel_sum.reshape(3, 3, chans, chans) * scale
    bias_grad = bias_sum[0] * scale
    return (outputs, input_grad, weight_grad, bias_grad)


def solution(mesh):
    in_specs = (P("lat", "lon", None), P(), P(), P("lat", "lon", None))
    out_specs = (P("lat", "lon", None), P("lat", "lon", None), P(), P())
    return jax.shard_map(shards, mesh=mesh, in_specs=in_specs, out_specs=out_specs, check_vma=False)
```

```python
import jax
import jax.numpy as jnp
from jax import lax
from jax.sharding import PartitionSpec as P


def extended(cells, sides, width, closed):
    for axis, dim in sides:
        count = lax.axis_size(axis)
        ends = count if closed else count - 1
        head = lax.slice_in_dim(cells, 0, width, axis=dim)
        tail = lax.slice_in_dim(cells, cells.shape[dim] - width, cells.shape[dim], axis=dim)
        cells = jnp.concatenate(
            [
                lax.ppermute(tail, axis, [(i, (i + 1) % count) for i in range(ends)]),
                cells,
                lax.ppermute(head, axis, [((i + 1) % count, i) for i in range(ends)]),
            ],
            axis=dim,
        )
    return cells


def from_behind(value, axis, steps):
    count = lax.axis_size(axis)
    pairs = [(source, (source + steps) % count) for source in range(count)]
    return lax.ppermute(value, axis, pairs)


def butterfly_sum(value, scatter, double, rider):
    shape = value.shape
    data = value.reshape(-1)
    parts = 2 ** len(scatter)
    pad = (-data.shape[0]) % parts
    data = jnp.pad(data, (0, pad))
    history = []
    for axis, step in scatter:
        count = lax.axis_size(axis)
        bit = (lax.axis_index(axis) // step) % 2
        half = data.shape[0] // 2
        pairs = [(i, i ^ step) for i in range(count)]
        send = lax.dynamic_slice_in_dim(data, (1 - bit) * half, half)
        keep = lax.dynamic_slice_in_dim(data, bit * half, half)
        data = keep + lax.ppermute(send, axis, pairs)
        history.append((axis, step, bit))
    data, rider = lax.optimization_barrier((data, rider))
    for axis, pairs in double:
        data = data + lax.ppermute(data, axis, pairs)
    for axis, step, bit in reversed(history):
        count = lax.axis_size(axis)
        pairs = [(i, i ^ step) for i in range(count)]
        other = lax.ppermute(data, axis, pairs)
        data = jnp.where(bit == 0, jnp.concatenate([data, other]), jnp.concatenate([other, data]))
    return data[: data.shape[0] - pad].reshape(shape), rider


def pairing_order(mesh_axes):
    near = []
    for axis in mesh_axes:
        step = 1
        while step < lax.axis_size(axis):
            near.append((axis, step))
            step *= 2
    ranked = [("lon", 1), ("lat", 1), ("lon", 4), ("lat", 2)]
    first = [pair for pair in ranked if pair in near]
    rest = [pair for pair in near if pair not in first]
    return first + rest


def reflected_ring_pairs(count, stride, size):
    pairs = []
    for i in range(count):
        z = (i // stride) % size
        if z % 2 == 0:
            w = (size - 2 - z) % size
        else:
            w = (size - z) % size
        pairs.append((i, i + (w - z) * stride))
    return pairs


def doubling_plan(rest):
    plan = []
    lon = lax.axis_size("lon")
    for axis, step in rest:
        count = lax.axis_size(axis)
        pairs = [(i, i ^ step) for i in range(count)]
        if axis == "lat" and step == 4 and count == 8:
            pairs = [(i, (3 - i // 2) * 2 + i % 2) for i in range(count)]
        if axis == "lon" and step == 16 and count == 32:
            pairs = reflected_ring_pairs(lon, 4, 8)
        plan.append((axis, pairs))
    return plan


def shards(inputs, weight, bias, cotangent):
    rows, cols, chans = inputs.shape
    band = lax.axis_index("lat")
    bands = lax.axis_size("lat")
    half = lax.axis_size("lon") // 2
    both = jnp.concatenate([inputs, cotangent], axis=2)
    wide = extended(both, (("lon", 1),), 2, True)
    tall = extended(wide, (("lat", 0),), 2, False)
    far = from_behind(jnp.stack([wide[0], wide[1], wide[-2], wide[-1]]), "lon", half)
    tall = tall.at[1].set(jnp.where(band == 0, far[0], tall[1]))
    tall = tall.at[rows + 2].set(jnp.where(band == bands - 1, far[3], tall[rows + 2]))
    padded = tall[:, :, :chans]
    ring_cot = tall[1:-1, 1:-1, chans:].astype(jnp.float32)
    pre = lax.conv_general_dilated(
        padded[None],
        weight,
        (1, 1),
        "VALID",
        dimension_numbers=("NHWC", "HWIO", "NHWC"),
        preferred_element_type=jnp.float32,
    )[0] + bias
    sig = jax.nn.sigmoid(pre)
    outputs = (pre * sig)[1:-1, 1:-1].astype(jnp.bfloat16)
    grad_ext = (ring_cot * sig * (1.0 + pre * (1.0 - sig))).astype(jnp.bfloat16)
    line = lax.broadcasted_iota(jnp.int32, (rows + 2, 1, 1), 0)
    outside = ((line == 0) & (band == 0)) | ((line == rows + 1) & (band == bands - 1))
    grad_ext = jnp.where(outside, jnp.zeros_like(grad_ext), grad_ext)
    pre_grad = grad_ext[1:-1, 1:-1].reshape(rows * cols, chans)
    taps = []
    for tap_a in range(3):
        for tap_b in range(3):
            window = padded[tap_a + 1 : tap_a + 1 + rows, tap_b + 1 : tap_b + 1 + cols].reshape(rows * cols, chans)
            taps.append(
                lax.dot_general(
                    window, pre_grad, (((0,), (0,)), ((), ())), preferred_element_type=jnp.float32
                )
            )
    kernel_terms = jnp.concatenate(taps, axis=0)
    bias_terms = jnp.sum(pre_grad.astype(jnp.float32), axis=0)[None, :]
    order = pairing_order(("lon", "lat"))
    sums, (grad_ext, wide_ends, far) = butterfly_sum(
        jnp.concatenate([kernel_terms, bias_terms], axis=0),
        order[:3],
        doubling_plan(order[3:]),
        (grad_ext, jnp.stack([wide[0], wide[-1]]), far),
    )
    flipped = jnp.transpose(weight[::-1, ::-1], (0, 1, 3, 2))
    cell_grad = lax.conv_general_dilated(
        grad_ext[None],
        flipped,
        (1, 1),
        "VALID",
        dimension_numbers=("NHWC", "HWIO", "NHWC"),
        preferred_element_type=jnp.float32,
    )[0]
    polar = []
    for window, cot_line, tap_a in (
        (jnp.stack([wide_ends[0], far[0], far[1]]), far[0], 0),
        (jnp.stack([far[2], far[3], wide_ends[1]]), far[3], 2),
    ):
        pre_line = bias + jnp.zeros((cols + 2, chans), jnp.float32)
        for tap_a_in in range(3):
            for tap_b_in in range(3):
                pre_line = pre_line + jnp.dot(
                    window[tap_a_in, tap_b_in : tap_b_in + cols + 2, :chans],
                    weight[tap_a_in, tap_b_in],
                    preferred_element_type=jnp.float32,
                )
        sig_line = jax.nn.sigmoid(pre_line)
        cot_far = cot_line[1:-1, chans:].astype(jnp.float32)
        grad_line = (cot_far * sig_line * (1.0 + pre_line * (1.0 - sig_line))).astype(jnp.bfloat16)
        ring = jnp.zeros((cols, chans), jnp.float32)
        for tap_b in range(3):
            ring = ring + jnp.dot(
                grad_line[tap_b : tap_b + cols],
                weight[tap_a, 2 - tap_b].T,
                preferred_element_type=jnp.float32,
            )
        polar.append(ring)
    cell_grad = cell_grad.at[0].add(jnp.where(band == 0, polar[0], 0.0))
    cell_grad = cell_grad.at[-1].add(jnp.where(band == bands - 1, polar[1], 0.0))
    input_grad = cell_grad.astype(jnp.bfloat16)
    kernel_sum, bias_sum = sums[:-1], sums[-1:]
    total_cells = rows * cols * lax.axis_size("lon") * lax.axis_size("lat")
    scale = 1.0 / jnp.sqrt(jnp.float32(total_cells))
    weight_grad = kernel_sum.reshape(3, 3, chans, chans) * scale
    bias_grad = bias_sum[0] * scale
    return (outputs, input_grad, weight_grad, bias_grad)


def solution(mesh):
    in_specs = (P("lat", "lon", None), P(), P(), P("lat", "lon", None))
    out_specs = (P("lat", "lon", None), P("lat", "lon", None), P(), P())
    return jax.shard_map(shards, mesh=mesh, in_specs=in_specs, out_specs=out_specs, check_vma=False)
```

```python
import jax
import jax.numpy as jnp
from jax import lax
from jax.sharding import PartitionSpec as P


def extended(cells, sides, width, closed):
    for axis, dim in sides:
        count = lax.axis_size(axis)
        ends = count if closed else count - 1
        head = lax.slice_in_dim(cells, 0, width, axis=dim)
        tail = lax.slice_in_dim(cells, cells.shape[dim] - width, cells.shape[dim], axis=dim)
        cells = jnp.concatenate(
            [
                lax.ppermute(tail, axis, [(i, (i + 1) % count) for i in range(ends)]),
                cells,
                lax.ppermute(head, axis, [((i + 1) % count, i) for i in range(ends)]),
            ],
            axis=dim,
        )
    return cells


def from_behind(value, axis, steps):
    count = lax.axis_size(axis)
    pairs = [(source, (source + steps) % count) for source in range(count)]
    return lax.ppermute(value, axis, pairs)


def butterfly_sum(value, scatter, double):
    shape = value.shape
    data = value.reshape(-1)
    parts = 2 ** len(scatter)
    pad = (-data.shape[0]) % parts
    data = jnp.pad(data, (0, pad))
    history = []
    for axis, step in scatter:
        count = lax.axis_size(axis)
        bit = (lax.axis_index(axis) // step) % 2
        half = data.shape[0] // 2
        pairs = [(i, i ^ step) for i in range(count)]
        send = lax.dynamic_slice_in_dim(data, (1 - bit) * half, half)
        keep = lax.dynamic_slice_in_dim(data, bit * half, half)
        data = keep + lax.ppermute(send, axis, pairs)
        history.append((axis, step, bit))
    for axis, pairs in double:
        data = data + lax.ppermute(data, axis, pairs)
    for axis, step, bit in reversed(history):
        count = lax.axis_size(axis)
        pairs = [(i, i ^ step) for i in range(count)]
        other = lax.ppermute(data, axis, pairs)
        data = jnp.where(bit == 0, jnp.concatenate([data, other]), jnp.concatenate([other, data]))
    return data[: data.shape[0] - pad].reshape(shape)


def pairing_order(mesh_axes):
    near = []
    for axis in mesh_axes:
        step = 1
        while step < lax.axis_size(axis):
            near.append((axis, step))
            step *= 2
    ranked = [("lon", 1), ("lat", 1), ("lon", 4), ("lat", 2)]
    first = [pair for pair in ranked if pair in near]
    rest = [pair for pair in near if pair not in first]
    return first + rest


def reflected_ring_pairs(count, stride, size):
    pairs = []
    for i in range(count):
        z = (i // stride) % size
        if z % 2 == 0:
            w = (size - 2 - z) % size
        else:
            w = (size - z) % size
        pairs.append((i, i + (w - z) * stride))
    return pairs


def doubling_plan(rest):
    plan = []
    lon = lax.axis_size("lon")
    for axis, step in rest:
        count = lax.axis_size(axis)
        pairs = [(i, i ^ step) for i in range(count)]
        if axis == "lat" and step == 4 and count == 8:
            pairs = [(i, (3 - i // 2) * 2 + i % 2) for i in range(count)]
        if axis == "lon" and step == 16 and count == 32:
            pairs = reflected_ring_pairs(lon, 4, 8)
        plan.append((axis, pairs))
    return plan


def shards(inputs, weight, bias, cotangent):
    rows, cols, chans = inputs.shape
    band = lax.axis_index("lat")
    bands = lax.axis_size("lat")
    half = lax.axis_size("lon") // 2
    both = jnp.concatenate([inputs, cotangent], axis=2)
    tall = extended(both, (("lat", 0),), 2, False)
    far = from_behind(jnp.stack([both[0], both[-1]]), "lon", half)
    tall = tall.at[1].set(jnp.where(band == 0, far[0], tall[1]))
    tall = tall.at[rows + 2].set(jnp.where(band == bands - 1, far[1], tall[rows + 2]))
    tall = extended(tall, (("lon", 1),), 2, True)
    padded = tall[:, :, :chans]
    ring_cot = tall[1:-1, 1:-1, chans:].astype(jnp.float32)
    pre = lax.conv_general_dilated(
        padded[None],
        weight,
        (1, 1),
        "VALID",
        dimension_numbers=("NHWC", "HWIO", "NHWC"),
        preferred_element_type=jnp.float32,
    )[0] + bias
    sig = jax.nn.sigmoid(pre)
    outputs = (pre * sig)[1:-1, 1:-1].astype(jnp.bfloat16)
    grad_ext = (ring_cot * sig * (1.0 + pre * (1.0 - sig))).astype(jnp.bfloat16)
    line = lax.broadcasted_iota(jnp.int32, (rows + 2, 1, 1), 0)
    outside = ((line == 0) & (band == 0)) | ((line == rows + 1) & (band == bands - 1))
    grad_ext = jnp.where(outside, jnp.zeros_like(grad_ext), grad_ext)
    pre_grad = grad_ext[1:-1, 1:-1].reshape(rows * cols, chans)
    flipped = jnp.transpose(weight[::-1, ::-1], (0, 1, 3, 2))
    cell_grad = lax.conv_general_dilated(
        grad_ext[None],
        flipped,
        (1, 1),
        "VALID",
        dimension_numbers=("NHWC", "HWIO", "NHWC"),
        preferred_element_type=jnp.float32,
    )[0]
    polar = []
    for line_at, tap_a in ((1, 0), (rows, 2)):
        ring = jnp.zeros((cols, chans), jnp.float32)
        for tap_b in range(3):
            ring = ring + jnp.dot(
                grad_ext[line_at, tap_b : tap_b + cols],
                weight[tap_a, 2 - tap_b].T,
                preferred_element_type=jnp.float32,
            )
        polar.append(ring)
    polar_in = from_behind(jnp.stack(polar).astype(jnp.bfloat16), "lon", half).astype(jnp.float32)
    cell_grad = cell_grad.at[0].add(jnp.where(band == 0, polar_in[0], 0.0))
    cell_grad = cell_grad.at[-1].add(jnp.where(band == bands - 1, polar_in[1], 0.0))
    input_grad = cell_grad.astype(jnp.bfloat16)
    taps = []
    for tap_a in range(3):
        for tap_b in range(3):
            window = padded[tap_a + 1 : tap_a + 1 + rows, tap_b + 1 : tap_b + 1 + cols].reshape(rows * cols, chans)
            taps.append(
                lax.dot_general(
                    window, pre_grad, (((0,), (0,)), ((), ())), preferred_element_type=jnp.float32
                )
            )
    kernel_terms = jnp.concatenate(taps, axis=0)
    bias_terms = jnp.sum(pre_grad.astype(jnp.float32), axis=0)[None, :]
    order = pairing_order(("lon", "lat"))
    sums = butterfly_sum(jnp.concatenate([kernel_terms, bias_terms], axis=0), order[:3], doubling_plan(order[3:]))
    kernel_sum, bias_sum = sums[:-1], sums[-1:]
    total_cells = rows * cols * lax.axis_size("lon") * lax.axis_size("lat")
    scale = 1.0 / jnp.sqrt(jnp.float32(total_cells))
    weight_grad = kernel_sum.reshape(3, 3, chans, chans) * scale
    bias_grad = bias_sum[0] * scale
    return (outputs, input_grad, weight_grad, bias_grad)


def solution(mesh):
    in_specs = (P("lat", "lon", None), P(), P(), P("lat", "lon", None))
    out_specs = (P("lat", "lon", None), P("lat", "lon", None), P(), P())
    return jax.shard_map(shards, mesh=mesh, in_specs=in_specs, out_specs=out_specs, check_vma=False)
```

```python
import jax
import jax.numpy as jnp
from jax import lax
from jax.sharding import PartitionSpec as P


def extended(cells, sides, width, closed):
    for axis, dim in sides:
        count = lax.axis_size(axis)
        ends = count if closed else count - 1
        head = lax.slice_in_dim(cells, 0, width, axis=dim)
        tail = lax.slice_in_dim(cells, cells.shape[dim] - width, cells.shape[dim], axis=dim)
        cells = jnp.concatenate(
            [
                lax.ppermute(tail, axis, [(i, (i + 1) % count) for i in range(ends)]),
                cells,
                lax.ppermute(head, axis, [((i + 1) % count, i) for i in range(ends)]),
            ],
            axis=dim,
        )
    return cells


def from_behind(value, axis, steps):
    count = lax.axis_size(axis)
    pairs = [(source, (source + steps) % count) for source in range(count)]
    return lax.ppermute(value, axis, pairs)


def butterfly_sum(value, scatter, double):
    shape = value.shape
    data = value.reshape(-1)
    parts = 2 ** len(scatter)
    pad = (-data.shape[0]) % parts
    data = jnp.pad(data, (0, pad))
    history = []
    for axis, step in scatter:
        count = lax.axis_size(axis)
        bit = (lax.axis_index(axis) // step) % 2
        half = data.shape[0] // 2
        pairs = [(i, i ^ step) for i in range(count)]
        send = lax.dynamic_slice_in_dim(data, (1 - bit) * half, half)
        keep = lax.dynamic_slice_in_dim(data, bit * half, half)
        data = keep + lax.ppermute(send, axis, pairs)
        history.append((axis, step, bit))
    for axis, pairs in double:
        data = data + lax.ppermute(data, axis, pairs)
    for axis, step, bit in reversed(history):
        count = lax.axis_size(axis)
        pairs = [(i, i ^ step) for i in range(count)]
        other = lax.ppermute(data, axis, pairs)
        data = jnp.where(bit == 0, jnp.concatenate([data, other]), jnp.concatenate([other, data]))
    return data[: data.shape[0] - pad].reshape(shape)


def pairing_order(mesh_axes):
    near = []
    for axis in mesh_axes:
        step = 1
        while step < lax.axis_size(axis):
            near.append((axis, step))
            step *= 2
    ranked = [("lon", 1), ("lat", 1), ("lon", 4), ("lat", 2)]
    first = [pair for pair in ranked if pair in near]
    rest = [pair for pair in near if pair not in first]
    return first + rest


def reflected_ring_pairs(count, stride, size):
    pairs = []
    for i in range(count):
        z = (i // stride) % size
        if z % 2 == 0:
            w = (size - 2 - z) % size
        else:
            w = (size - z) % size
        pairs.append((i, i + (w - z) * stride))
    return pairs


def doubling_plan(rest):
    plan = []
    lon = lax.axis_size("lon")
    for axis, step in rest:
        count = lax.axis_size(axis)
        pairs = [(i, i ^ step) for i in range(count)]
        if axis == "lat" and step == 4 and count == 8:
            pairs = [(i, (3 - i // 2) * 2 + i % 2) for i in range(count)]
        if axis == "lon" and step == 16 and count == 32:
            pairs = reflected_ring_pairs(lon, 4, 8)
        plan.append((axis, pairs))
    return plan


def shards(inputs, weight, bias, cotangent):
    rows, cols, chans = inputs.shape
    band = lax.axis_index("lat")
    bands = lax.axis_size("lat")
    half = lax.axis_size("lon") // 2
    both = jnp.concatenate([inputs, cotangent], axis=2)
    wide = extended(both, (("lon", 1),), 2, True)
    tall = extended(wide, (("lat", 0),), 2, False)
    far = from_behind(jnp.stack([wide[0], wide[-1]]), "lon", half)
    tall = tall.at[1].set(jnp.where(band == 0, far[0], tall[1]))
    tall = tall.at[rows + 2].set(jnp.where(band == bands - 1, far[1], tall[rows + 2]))
    padded = tall[:, :, :chans]
    ring_cot = tall[1:-1, 1:-1, chans:].astype(jnp.float32)
    pre = lax.conv_general_dilated(
        padded[None],
        weight,
        (1, 1),
        "VALID",
        dimension_numbers=("NHWC", "HWIO", "NHWC"),
        preferred_element_type=jnp.float32,
    )[0] + bias
    sig = jax.nn.sigmoid(pre)
    outputs = (pre * sig)[1:-1, 1:-1].astype(jnp.bfloat16)
    grad_ext = (ring_cot * sig * (1.0 + pre * (1.0 - sig))).astype(jnp.bfloat16)
    line = lax.broadcasted_iota(jnp.int32, (rows + 2, 1, 1), 0)
    outside = ((line == 0) & (band == 0)) | ((line == rows + 1) & (band == bands - 1))
    grad_ext = jnp.where(outside, jnp.zeros_like(grad_ext), grad_ext)
    pre_grad = grad_ext[1:-1, 1:-1].reshape(rows * cols, chans)
    flipped = jnp.transpose(weight[::-1, ::-1], (0, 1, 3, 2))
    cell_grad = lax.conv_general_dilated(
        grad_ext[None],
        flipped,
        (1, 1),
        "VALID",
        dimension_numbers=("NHWC", "HWIO", "NHWC"),
        preferred_element_type=jnp.float32,
    )[0]
    polar = []
    for line_at, tap_a in ((1, 0), (rows, 2)):
        ring = jnp.zeros((cols, chans), jnp.float32)
        for tap_b in range(3):
            ring = ring + jnp.dot(
                grad_ext[line_at, tap_b : tap_b + cols],
                weight[tap_a, 2 - tap_b].T,
                preferred_element_type=jnp.float32,
            )
        polar.append(ring)
    polar_in = from_behind(jnp.stack(polar).astype(jnp.bfloat16), "lon", half).astype(jnp.float32)
    taps = []
    for tap_a in range(3):
        for tap_b in range(3):
            window = padded[tap_a + 1 : tap_a + 1 + rows, tap_b + 1 : tap_b + 1 + cols].reshape(rows * cols, chans)
            taps.append(
                lax.dot_general(
                    window, pre_grad, (((0,), (0,)), ((), ())), preferred_element_type=jnp.float32
                )
            )
    kernel_terms = jnp.concatenate(taps, axis=0)
    bias_terms = jnp.sum(pre_grad.astype(jnp.float32), axis=0)[None, :]
    order = pairing_order(("lon", "lat"))
    terms, polar_in = lax.optimization_barrier((jnp.concatenate([kernel_terms, bias_terms], axis=0), polar_in))
    sums = butterfly_sum(terms, order[:3], doubling_plan(order[3:]))
    kernel_sum, bias_sum = sums[:-1], sums[-1:]
    cell_grad = cell_grad.at[0].add(jnp.where(band == 0, polar_in[0], 0.0))
    cell_grad = cell_grad.at[-1].add(jnp.where(band == bands - 1, polar_in[1], 0.0))
    input_grad = cell_grad.astype(jnp.bfloat16)

    total_cells = rows * cols * lax.axis_size("lon") * lax.axis_size("lat")
    scale = 1.0 / jnp.sqrt(jnp.float32(total_cells))
    weight_grad = kernel_sum.reshape(3, 3, chans, chans) * scale
    bias_grad = bias_sum[0] * scale
    return (outputs, input_grad, weight_grad, bias_grad)


def solution(mesh):
    in_specs = (P("lat", "lon", None), P(), P(), P("lat", "lon", None))
    out_specs = (P("lat", "lon", None), P("lat", "lon", None), P(), P())
    return jax.shard_map(shards, mesh=mesh, in_specs=in_specs, out_specs=out_specs, check_vma=False)
```

```python
import jax
import jax.numpy as jnp
from jax import lax
from jax.sharding import PartitionSpec as P


def extended(cells, sides, width, closed):
    for axis, dim in sides:
        count = lax.axis_size(axis)
        ends = count if closed else count - 1
        head = lax.slice_in_dim(cells, 0, width, axis=dim)
        tail = lax.slice_in_dim(cells, cells.shape[dim] - width, cells.shape[dim], axis=dim)
        cells = jnp.concatenate(
            [
                lax.ppermute(tail, axis, [(i, (i + 1) % count) for i in range(ends)]),
                cells,
                lax.ppermute(head, axis, [((i + 1) % count, i) for i in range(ends)]),
            ],
            axis=dim,
        )
    return cells


def from_behind(value, axis, steps):
    count = lax.axis_size(axis)
    pairs = [(source, (source + steps) % count) for source in range(count)]
    return lax.ppermute(value, axis, pairs)


def butterfly_sum(value, scatter, double):
    shape = value.shape
    data = value.reshape(-1)
    parts = 2 ** len(scatter)
    pad = (-data.shape[0]) % parts
    data = jnp.pad(data, (0, pad))
    history = []
    for axis, step in scatter:
        count = lax.axis_size(axis)
        bit = (lax.axis_index(axis) // step) % 2
        half = data.shape[0] // 2
        pairs = [(i, i ^ step) for i in range(count)]
        send = lax.dynamic_slice_in_dim(data, (1 - bit) * half, half)
        keep = lax.dynamic_slice_in_dim(data, bit * half, half)
        data = keep + lax.ppermute(send, axis, pairs)
        history.append((axis, step, bit))
    for axis, pairs in double:
        data = data + lax.ppermute(data, axis, pairs)
    for axis, step, bit in reversed(history):
        count = lax.axis_size(axis)
        pairs = [(i, i ^ step) for i in range(count)]
        other = lax.ppermute(data, axis, pairs)
        data = jnp.where(bit == 0, jnp.concatenate([data, other]), jnp.concatenate([other, data]))
    return data[: data.shape[0] - pad].reshape(shape)


def pairing_order(mesh_axes):
    near = []
    for axis in mesh_axes:
        step = 1
        while step < lax.axis_size(axis):
            near.append((axis, step))
            step *= 2
    ranked = [("lon", 1), ("lon", 4), ("lat", 1), ("lat", 2)]
    first = [pair for pair in ranked if pair in near]
    rest = [pair for pair in near if pair not in first]
    return first + rest


def reflected_ring_pairs(count, stride, size):
    pairs = []
    for i in range(count):
        z = (i // stride) % size
        if z % 2 == 0:
            w = (size - 2 - z) % size
        else:
            w = (size - z) % size
        pairs.append((i, i + (w - z) * stride))
    return pairs


def doubling_plan(rest):
    plan = []
    lon = lax.axis_size("lon")
    for axis, step in rest:
        count = lax.axis_size(axis)
        pairs = [(i, i ^ step) for i in range(count)]
        if axis == "lat" and step == 4 and count == 8:
            pairs = [(i, (3 - i // 2) * 2 + i % 2) for i in range(count)]
        if axis == "lon" and step == 16 and count == 32:
            pairs = reflected_ring_pairs(lon, 4, 8)
        plan.append((axis, pairs))
    return plan


def shards(inputs, weight, bias, cotangent):
    rows, cols, chans = inputs.shape
    band = lax.axis_index("lat")
    bands = lax.axis_size("lat")
    half = lax.axis_size("lon") // 2
    both = jnp.concatenate([inputs, cotangent], axis=2)
    wide = extended(both, (("lon", 1),), 2, True)
    tall = extended(wide, (("lat", 0),), 2, False)
    far = from_behind(jnp.stack([wide[0], wide[-1]]), "lon", half)
    tall = tall.at[1].set(jnp.where(band == 0, far[0], tall[1]))
    tall = tall.at[rows + 2].set(jnp.where(band == bands - 1, far[1], tall[rows + 2]))
    padded = tall[:, :, :chans]
    ring_cot = tall[1:-1, 1:-1, chans:].astype(jnp.float32)
    pre = lax.conv_general_dilated(
        padded[None],
        weight,
        (1, 1),
        "VALID",
        dimension_numbers=("NHWC", "HWIO", "NHWC"),
        preferred_element_type=jnp.float32,
    )[0] + bias
    sig = jax.nn.sigmoid(pre)
    outputs = (pre * sig)[1:-1, 1:-1].astype(jnp.bfloat16)
    grad_ext = (ring_cot * sig * (1.0 + pre * (1.0 - sig))).astype(jnp.bfloat16)
    line = lax.broadcasted_iota(jnp.int32, (rows + 2, 1, 1), 0)
    outside = ((line == 0) & (band == 0)) | ((line == rows + 1) & (band == bands - 1))
    grad_ext = jnp.where(outside, jnp.zeros_like(grad_ext), grad_ext)
    pre_grad = grad_ext[1:-1, 1:-1].reshape(rows * cols, chans)
    flipped = jnp.transpose(weight[::-1, ::-1], (0, 1, 3, 2))
    cell_grad = lax.conv_general_dilated(
        grad_ext[None],
        flipped,
        (1, 1),
        "VALID",
        dimension_numbers=("NHWC", "HWIO", "NHWC"),
        preferred_element_type=jnp.float32,
    )[0]
    polar = []
    for line_at, tap_a in ((1, 0), (rows, 2)):
        ring = jnp.zeros((cols, chans), jnp.float32)
        for tap_b in range(3):
            ring = ring + jnp.dot(
                grad_ext[line_at, tap_b : tap_b + cols],
                weight[tap_a, 2 - tap_b].T,
                preferred_element_type=jnp.float32,
            )
        polar.append(ring)
    polar_in = from_behind(jnp.stack(polar).astype(jnp.bfloat16), "lon", half).astype(jnp.float32)
    cell_grad = cell_grad.at[0].add(jnp.where(band == 0, polar_in[0], 0.0))
    cell_grad = cell_grad.at[-1].add(jnp.where(band == bands - 1, polar_in[1], 0.0))
    input_grad = cell_grad.astype(jnp.bfloat16)
    taps = []
    for tap_a in range(3):
        for tap_b in range(3):
            window = padded[tap_a + 1 : tap_a + 1 + rows, tap_b + 1 : tap_b + 1 + cols].reshape(rows * cols, chans)
            taps.append(
                lax.dot_general(
                    window, pre_grad, (((0,), (0,)), ((), ())), preferred_element_type=jnp.float32
                )
            )
    kernel_terms = jnp.concatenate(taps, axis=0)
    bias_terms = jnp.sum(pre_grad.astype(jnp.float32), axis=0)[None, :]
    order = pairing_order(("lon", "lat"))
    sums = butterfly_sum(jnp.concatenate([kernel_terms, bias_terms], axis=0), order[:3], doubling_plan(order[3:]))
    kernel_sum, bias_sum = sums[:-1], sums[-1:]
    total_cells = rows * cols * lax.axis_size("lon") * lax.axis_size("lat")
    scale = 1.0 / jnp.sqrt(jnp.float32(total_cells))
    weight_grad = kernel_sum.reshape(3, 3, chans, chans) * scale
    bias_grad = bias_sum[0] * scale
    return (outputs, input_grad, weight_grad, bias_grad)


def solution(mesh):
    in_specs = (P("lat", "lon", None), P(), P(), P("lat", "lon", None))
    out_specs = (P("lat", "lon", None), P("lat", "lon", None), P(), P())
    return jax.shard_map(shards, mesh=mesh, in_specs=in_specs, out_specs=out_specs, check_vma=False)
```

```python
import jax
import jax.numpy as jnp
from jax import lax
from jax.sharding import PartitionSpec as P


def extended(cells, sides, width, closed):
    for axis, dim in sides:
        count = lax.axis_size(axis)
        ends = count if closed else count - 1
        head = lax.slice_in_dim(cells, 0, width, axis=dim)
        tail = lax.slice_in_dim(cells, cells.shape[dim] - width, cells.shape[dim], axis=dim)
        cells = jnp.concatenate(
            [
                lax.ppermute(tail, axis, [(i, (i + 1) % count) for i in range(ends)]),
                cells,
                lax.ppermute(head, axis, [((i + 1) % count, i) for i in range(ends)]),
            ],
            axis=dim,
        )
    return cells


def from_behind(value, axis, steps):
    count = lax.axis_size(axis)
    pairs = [(source, (source + steps) % count) for source in range(count)]
    return lax.ppermute(value, axis, pairs)


def polar_behind(value, steps):
    count = lax.axis_size("lon")
    bands = lax.axis_size("lat")
    pairs = []
    for band in sorted({0, bands - 1}):
        for source in range(count):
            pairs.append((source * bands + band, ((source + steps) % count) * bands + band))
    return lax.ppermute(value, ("lon", "lat"), pairs)


def butterfly_sum(value, scatter, double):
    shape = value.shape
    data = value.reshape(-1)
    parts = 2 ** len(scatter)
    pad = (-data.shape[0]) % parts
    data = jnp.pad(data, (0, pad))
    history = []
    for axis, step in scatter:
        count = lax.axis_size(axis)
        bit = (lax.axis_index(axis) // step) % 2
        half = data.shape[0] // 2
        pairs = [(i, i ^ step) for i in range(count)]
        send = lax.dynamic_slice_in_dim(data, (1 - bit) * half, half)
        keep = lax.dynamic_slice_in_dim(data, bit * half, half)
        data = keep + lax.ppermute(send, axis, pairs)
        history.append((axis, step, bit))
    for axis, pairs in double:
        data = data + lax.ppermute(data, axis, pairs)
    for axis, step, bit in reversed(history):
        count = lax.axis_size(axis)
        pairs = [(i, i ^ step) for i in range(count)]
        other = lax.ppermute(data, axis, pairs)
        data = jnp.where(bit == 0, jnp.concatenate([data, other]), jnp.concatenate([other, data]))
    return data[: data.shape[0] - pad].reshape(shape)


def pairing_order(mesh_axes):
    near = []
    for axis in mesh_axes:
        step = 1
        while step < lax.axis_size(axis):
            near.append((axis, step))
            step *= 2
    ranked = [("lon", 1), ("lat", 1), ("lon", 4), ("lat", 2)]
    first = [pair for pair in ranked if pair in near]
    rest = [pair for pair in near if pair not in first]
    return first + rest


def reflected_ring_pairs(count, stride, size):
    pairs = []
    for i in range(count):
        z = (i // stride) % size
        if z % 2 == 0:
            w = (size - 2 - z) % size
        else:
            w = (size - z) % size
        pairs.append((i, i + (w - z) * stride))
    return pairs


def doubling_plan(rest):
    plan = []
    lon = lax.axis_size("lon")
    for axis, step in rest:
        count = lax.axis_size(axis)
        pairs = [(i, i ^ step) for i in range(count)]
        if axis == "lat" and step == 4 and count == 8:
            pairs = [(i, (3 - i // 2) * 2 + i % 2) for i in range(count)]
        if axis == "lon" and step == 16 and count == 32:
            pairs = reflected_ring_pairs(lon, 4, 8)
        plan.append((axis, pairs))
    return plan


def shards(inputs, weight, bias, cotangent):
    rows, cols, chans = inputs.shape
    band = lax.axis_index("lat")
    bands = lax.axis_size("lat")
    half = lax.axis_size("lon") // 2
    both = jnp.concatenate([inputs, cotangent], axis=2)
    wide = extended(both, (("lon", 1),), 2, True)
    tall = extended(wide, (("lat", 0),), 2, False)
    far = polar_behind(jnp.stack([wide[0], wide[-1]]), half)
    tall = tall.at[1].set(jnp.where(band == 0, far[0], tall[1]))
    tall = tall.at[rows + 2].set(jnp.where(band == bands - 1, far[1], tall[rows + 2]))
    padded = tall[:, :, :chans]
    ring_cot = tall[1:-1, 1:-1, chans:].astype(jnp.float32)
    pre = lax.conv_general_dilated(
        padded[None],
        weight,
        (1, 1),
        "VALID",
        dimension_numbers=("NHWC", "HWIO", "NHWC"),
        preferred_element_type=jnp.float32,
    )[0] + bias
    sig = jax.nn.sigmoid(pre)
    outputs = (pre * sig)[1:-1, 1:-1].astype(jnp.bfloat16)
    grad_ext = (ring_cot * sig * (1.0 + pre * (1.0 - sig))).astype(jnp.bfloat16)
    line = lax.broadcasted_iota(jnp.int32, (rows + 2, 1, 1), 0)
    outside = ((line == 0) & (band == 0)) | ((line == rows + 1) & (band == bands - 1))
    grad_ext = jnp.where(outside, jnp.zeros_like(grad_ext), grad_ext)
    pre_grad = grad_ext[1:-1, 1:-1].reshape(rows * cols, chans)
    flipped = jnp.transpose(weight[::-1, ::-1], (0, 1, 3, 2))
    cell_grad = lax.conv_general_dilated(
        grad_ext[None],
        flipped,
        (1, 1),
        "VALID",
        dimension_numbers=("NHWC", "HWIO", "NHWC"),
        preferred_element_type=jnp.float32,
    )[0]
    polar = []
    for line_at, tap_a in ((1, 0), (rows, 2)):
        ring = jnp.zeros((cols, chans), jnp.float32)
        for tap_b in range(3):
            ring = ring + jnp.dot(
                grad_ext[line_at, tap_b : tap_b + cols],
                weight[tap_a, 2 - tap_b].T,
                preferred_element_type=jnp.float32,
            )
        polar.append(ring)
    polar_in = polar_behind(jnp.stack(polar).astype(jnp.bfloat16), half).astype(jnp.float32)
    cell_grad = cell_grad.at[0].add(jnp.where(band == 0, polar_in[0], 0.0))
    cell_grad = cell_grad.at[-1].add(jnp.where(band == bands - 1, polar_in[1], 0.0))
    input_grad = cell_grad.astype(jnp.bfloat16)
    taps = []
    for tap_a in range(3):
        for tap_b in range(3):
            window = padded[tap_a + 1 : tap_a + 1 + rows, tap_b + 1 : tap_b + 1 + cols].reshape(rows * cols, chans)
            taps.append(
                lax.dot_general(
                    window, pre_grad, (((0,), (0,)), ((), ())), preferred_element_type=jnp.float32
                )
            )
    kernel_terms = jnp.concatenate(taps, axis=0)
    bias_terms = jnp.sum(pre_grad.astype(jnp.float32), axis=0)[None, :]
    order = pairing_order(("lon", "lat"))
    sums = butterfly_sum(jnp.concatenate([kernel_terms, bias_terms], axis=0), order[:3], doubling_plan(order[3:]))
    kernel_sum, bias_sum = sums[:-1], sums[-1:]
    total_cells = rows * cols * lax.axis_size("lon") * lax.axis_size("lat")
    scale = 1.0 / jnp.sqrt(jnp.float32(total_cells))
    weight_grad = kernel_sum.reshape(3, 3, chans, chans) * scale
    bias_grad = bias_sum[0] * scale
    return (outputs, input_grad, weight_grad, bias_grad)


def solution(mesh):
    in_specs = (P("lat", "lon", None), P(), P(), P("lat", "lon", None))
    out_specs = (P("lat", "lon", None), P("lat", "lon", None), P(), P())
    return jax.shard_map(shards, mesh=mesh, in_specs=in_specs, out_specs=out_specs, check_vma=False)
```

```python
import jax
import jax.numpy as jnp
from jax import lax
from jax.sharding import PartitionSpec as P


def extended(cells, sides, width, closed):
    for axis, dim in sides:
        count = lax.axis_size(axis)
        ends = count if closed else count - 1
        head = lax.slice_in_dim(cells, 0, width, axis=dim)
        tail = lax.slice_in_dim(cells, cells.shape[dim] - width, cells.shape[dim], axis=dim)
        cells = jnp.concatenate(
            [
                lax.ppermute(tail, axis, [(i, (i + 1) % count) for i in range(ends)]),
                cells,
                lax.ppermute(head, axis, [((i + 1) % count, i) for i in range(ends)]),
            ],
            axis=dim,
        )
    return cells


def from_behind(value, axis, steps):
    count = lax.axis_size(axis)
    pairs = [(source, (source + steps) % count) for source in range(count)]
    return lax.ppermute(value, axis, pairs)


def butterfly_sum(value, scatter, double):
    shape = value.shape
    data = value.reshape(-1)
    parts = 2 ** len(scatter)
    pad = (-data.shape[0]) % parts
    data = jnp.pad(data, (0, pad))
    history = []
    for axis, step in scatter:
        count = lax.axis_size(axis)
        bit = (lax.axis_index(axis) // step) % 2
        half = data.shape[0] // 2
        pairs = [(i, i ^ step) for i in range(count)]
        send = lax.dynamic_slice_in_dim(data, (1 - bit) * half, half)
        keep = lax.dynamic_slice_in_dim(data, bit * half, half)
        data = keep + lax.ppermute(send, axis, pairs)
        history.append((axis, step, bit))
    for axis, pairs in double:
        data = data + lax.ppermute(data, axis, pairs)
    for axis, step, bit in reversed(history):
        count = lax.axis_size(axis)
        pairs = [(i, i ^ step) for i in range(count)]
        other = lax.ppermute(data, axis, pairs)
        whole = jnp.zeros((2 * data.shape[0],), data.dtype)
        whole = lax.dynamic_update_slice_in_dim(whole, data, bit * data.shape[0], 0)
        data = lax.dynamic_update_slice_in_dim(whole, other, (1 - bit) * data.shape[0], 0)
    return data[: data.shape[0] - pad].reshape(shape)


def pairing_order(mesh_axes):
    near = []
    for axis in mesh_axes:
        step = 1
        while step < lax.axis_size(axis):
            near.append((axis, step))
            step *= 2
    ranked = [("lon", 1), ("lat", 1), ("lon", 4), ("lat", 2)]
    first = [pair for pair in ranked if pair in near]
    rest = [pair for pair in near if pair not in first]
    return first + rest


def reflected_ring_pairs(count, stride, size):
    pairs = []
    for i in range(count):
        z = (i // stride) % size
        if z % 2 == 0:
            w = (size - 2 - z) % size
        else:
            w = (size - z) % size
        pairs.append((i, i + (w - z) * stride))
    return pairs


def doubling_plan(rest):
    plan = []
    lon = lax.axis_size("lon")
    for axis, step in rest:
        count = lax.axis_size(axis)
        pairs = [(i, i ^ step) for i in range(count)]
        if axis == "lat" and step == 4 and count == 8:
            pairs = [(i, (3 - i // 2) * 2 + i % 2) for i in range(count)]
        if axis == "lon" and step == 16 and count == 32:
            pairs = reflected_ring_pairs(lon, 4, 8)
        plan.append((axis, pairs))
    return plan


def shards(inputs, weight, bias, cotangent):
    rows, cols, chans = inputs.shape
    band = lax.axis_index("lat")
    bands = lax.axis_size("lat")
    half = lax.axis_size("lon") // 2
    both = jnp.concatenate([inputs, cotangent], axis=2)
    wide = extended(both, (("lon", 1),), 2, True)
    tall = extended(wide, (("lat", 0),), 2, False)
    far = from_behind(jnp.stack([wide[0], wide[-1]]), "lon", half)
    tall = tall.at[1].set(jnp.where(band == 0, far[0], tall[1]))
    tall = tall.at[rows + 2].set(jnp.where(band == bands - 1, far[1], tall[rows + 2]))
    padded = tall[:, :, :chans]
    ring_cot = tall[1:-1, 1:-1, chans:].astype(jnp.float32)
    pre = lax.conv_general_dilated(
        padded[None],
        weight,
        (1, 1),
        "VALID",
        dimension_numbers=("NHWC", "HWIO", "NHWC"),
        preferred_element_type=jnp.float32,
    )[0] + bias
    sig = jax.nn.sigmoid(pre)
    outputs = (pre * sig)[1:-1, 1:-1].astype(jnp.bfloat16)
    grad_ext = (ring_cot * sig * (1.0 + pre * (1.0 - sig))).astype(jnp.bfloat16)
    line = lax.broadcasted_iota(jnp.int32, (rows + 2, 1, 1), 0)
    outside = ((line == 0) & (band == 0)) | ((line == rows + 1) & (band == bands - 1))
    grad_ext = jnp.where(outside, jnp.zeros_like(grad_ext), grad_ext)
    pre_grad = grad_ext[1:-1, 1:-1].reshape(rows * cols, chans)
    flipped = jnp.transpose(weight[::-1, ::-1], (0, 1, 3, 2))
    cell_grad = lax.conv_general_dilated(
        grad_ext[None],
        flipped,
        (1, 1),
        "VALID",
        dimension_numbers=("NHWC", "HWIO", "NHWC"),
        preferred_element_type=jnp.float32,
    )[0]
    polar = []
    for line_at, tap_a in ((1, 0), (rows, 2)):
        ring = jnp.zeros((cols, chans), jnp.float32)
        for tap_b in range(3):
            ring = ring + jnp.dot(
                grad_ext[line_at, tap_b : tap_b + cols],
                weight[tap_a, 2 - tap_b].T,
                preferred_element_type=jnp.float32,
            )
        polar.append(ring)
    polar_in = from_behind(jnp.stack(polar).astype(jnp.bfloat16), "lon", half).astype(jnp.float32)
    cell_grad = cell_grad.at[0].add(jnp.where(band == 0, polar_in[0], 0.0))
    cell_grad = cell_grad.at[-1].add(jnp.where(band == bands - 1, polar_in[1], 0.0))
    input_grad = cell_grad.astype(jnp.bfloat16)
    taps = []
    for tap_a in range(3):
        for tap_b in range(3):
            window = padded[tap_a + 1 : tap_a + 1 + rows, tap_b + 1 : tap_b + 1 + cols].reshape(rows * cols, chans)
            taps.append(
                lax.dot_general(
                    window, pre_grad, (((0,), (0,)), ((), ())), preferred_element_type=jnp.float32
                )
            )
    kernel_terms = jnp.concatenate(taps, axis=0)
    bias_terms = jnp.sum(pre_grad.astype(jnp.float32), axis=0)[None, :]
    order = pairing_order(("lon", "lat"))
    sums = butterfly_sum(jnp.concatenate([kernel_terms, bias_terms], axis=0), order[:3], doubling_plan(order[3:]))
    kernel_sum, bias_sum = sums[:-1], sums[-1:]
    total_cells = rows * cols * lax.axis_size("lon") * lax.axis_size("lat")
    scale = 1.0 / jnp.sqrt(jnp.float32(total_cells))
    weight_grad = kernel_sum.reshape(3, 3, chans, chans) * scale
    bias_grad = bias_sum[0] * scale
    return (outputs, input_grad, weight_grad, bias_grad)


def solution(mesh):
    in_specs = (P("lat", "lon", None), P(), P(), P("lat", "lon", None))
    out_specs = (P("lat", "lon", None), P("lat", "lon", None), P(), P())
    return jax.shard_map(shards, mesh=mesh, in_specs=in_specs, out_specs=out_specs, check_vma=False)
```

```python
import jax
import jax.numpy as jnp
from jax import lax
from jax.sharding import PartitionSpec as P


def extended(cells, sides, width, closed):
    for axis, dim in sides:
        count = lax.axis_size(axis)
        ends = count if closed else count - 1
        head = lax.slice_in_dim(cells, 0, width, axis=dim)
        tail = lax.slice_in_dim(cells, cells.shape[dim] - width, cells.shape[dim], axis=dim)
        cells = jnp.concatenate(
            [
                lax.ppermute(tail, axis, [(i, (i + 1) % count) for i in range(ends)]),
                cells,
                lax.ppermute(head, axis, [((i + 1) % count, i) for i in range(ends)]),
            ],
            axis=dim,
        )
    return cells


def from_behind(value, axis, steps):
    count = lax.axis_size(axis)
    pairs = [(source, (source + steps) % count) for source in range(count)]
    return lax.ppermute(value, axis, pairs)


def butterfly_sum(value, scatter, double, rider):
    shape = value.shape
    data = value.reshape(-1)
    parts = 2 ** len(scatter)
    pad = (-data.shape[0]) % parts
    data = jnp.pad(data, (0, pad))
    history = []
    for axis, step in scatter:
        count = lax.axis_size(axis)
        bit = (lax.axis_index(axis) // step) % 2
        half = data.shape[0] // 2
        pairs = [(i, i ^ step) for i in range(count)]
        send = lax.dynamic_slice_in_dim(data, (1 - bit) * half, half)
        keep = lax.dynamic_slice_in_dim(data, bit * half, half)
        data = keep + lax.ppermute(send, axis, pairs)
        history.append((axis, step, bit))
    for axis, pairs in double:
        data = data + lax.ppermute(data, axis, pairs)
    data, rider = lax.optimization_barrier((data, rider))
    for axis, step, bit in reversed(history):
        count = lax.axis_size(axis)
        pairs = [(i, i ^ step) for i in range(count)]
        other = lax.ppermute(data, axis, pairs)
        data = jnp.where(bit == 0, jnp.concatenate([data, other]), jnp.concatenate([other, data]))
    return data[: data.shape[0] - pad].reshape(shape), rider


def pairing_order(mesh_axes):
    near = []
    for axis in mesh_axes:
        step = 1
        while step < lax.axis_size(axis):
            near.append((axis, step))
            step *= 2
    ranked = [("lon", 1), ("lat", 1), ("lon", 4), ("lat", 2)]
    first = [pair for pair in ranked if pair in near]
    rest = [pair for pair in near if pair not in first]
    return first + rest


def reflected_ring_pairs(count, stride, size):
    pairs = []
    for i in range(count):
        z = (i // stride) % size
        if z % 2 == 0:
            w = (size - 2 - z) % size
        else:
            w = (size - z) % size
        pairs.append((i, i + (w - z) * stride))
    return pairs


def doubling_plan(rest):
    plan = []
    lon = lax.axis_size("lon")
    for axis, step in rest:
        count = lax.axis_size(axis)
        pairs = [(i, i ^ step) for i in range(count)]
        if axis == "lat" and step == 4 and count == 8:
            pairs = [(i, (3 - i // 2) * 2 + i % 2) for i in range(count)]
        if axis == "lon" and step == 16 and count == 32:
            pairs = reflected_ring_pairs(lon, 4, 8)
        plan.append((axis, pairs))
    return plan


def shards(inputs, weight, bias, cotangent):
    rows, cols, chans = inputs.shape
    band = lax.axis_index("lat")
    bands = lax.axis_size("lat")
    half = lax.axis_size("lon") // 2
    both = jnp.concatenate([inputs, cotangent], axis=2)
    wide = extended(both, (("lon", 1),), 2, True)
    tall = extended(wide, (("lat", 0),), 2, False)
    far = from_behind(jnp.stack([wide[0], wide[-1]]), "lon", half)
    tall = tall.at[1].set(jnp.where(band == 0, far[0], tall[1]))
    tall = tall.at[rows + 2].set(jnp.where(band == bands - 1, far[1], tall[rows + 2]))
    padded = tall[:, :, :chans]
    ring_cot = tall[1:-1, 1:-1, chans:].astype(jnp.float32)
    pre = lax.conv_general_dilated(
        padded[None],
        weight,
        (1, 1),
        "VALID",
        dimension_numbers=("NHWC", "HWIO", "NHWC"),
        preferred_element_type=jnp.float32,
    )[0] + bias
    sig = jax.nn.sigmoid(pre)
    outputs = (pre * sig)[1:-1, 1:-1].astype(jnp.bfloat16)
    grad_ext = (ring_cot * sig * (1.0 + pre * (1.0 - sig))).astype(jnp.bfloat16)
    line = lax.broadcasted_iota(jnp.int32, (rows + 2, 1, 1), 0)
    outside = ((line == 0) & (band == 0)) | ((line == rows + 1) & (band == bands - 1))
    grad_ext = jnp.where(outside, jnp.zeros_like(grad_ext), grad_ext)
    pre_grad = grad_ext[1:-1, 1:-1].reshape(rows * cols, chans)
    flipped = jnp.transpose(weight[::-1, ::-1], (0, 1, 3, 2))
    cell_grad = lax.conv_general_dilated(
        grad_ext[None],
        flipped,
        (1, 1),
        "VALID",
        dimension_numbers=("NHWC", "HWIO", "NHWC"),
        preferred_element_type=jnp.float32,
    )[0]
    polar = []
    for line_at, tap_a in ((1, 0), (rows, 2)):
        ring = jnp.zeros((cols, chans), jnp.float32)
        for tap_b in range(3):
            ring = ring + jnp.dot(
                grad_ext[line_at, tap_b : tap_b + cols],
                weight[tap_a, 2 - tap_b].T,
                preferred_element_type=jnp.float32,
            )
        polar.append(ring)
    polar_out = jnp.stack(polar).astype(jnp.bfloat16)
    taps = []
    for tap_a in range(3):
        for tap_b in range(3):
            window = padded[tap_a + 1 : tap_a + 1 + rows, tap_b + 1 : tap_b + 1 + cols].reshape(rows * cols, chans)
            taps.append(
                lax.dot_general(
                    window, pre_grad, (((0,), (0,)), ((), ())), preferred_element_type=jnp.float32
                )
            )
    kernel_terms = jnp.concatenate(taps, axis=0)
    bias_terms = jnp.sum(pre_grad.astype(jnp.float32), axis=0)[None, :]
    order = pairing_order(("lon", "lat"))
    sums, polar_out = butterfly_sum(
        jnp.concatenate([kernel_terms, bias_terms], axis=0), order[:3], doubling_plan(order[3:]), polar_out
    )
    polar_in = from_behind(polar_out, "lon", half).astype(jnp.float32)
    cell_grad = cell_grad.at[0].add(jnp.where(band == 0, polar_in[0], 0.0))
    cell_grad = cell_grad.at[-1].add(jnp.where(band == bands - 1, polar_in[1], 0.0))
    input_grad = cell_grad.astype(jnp.bfloat16)
    kernel_sum, bias_sum = sums[:-1], sums[-1:]
    total_cells = rows * cols * lax.axis_size("lon") * lax.axis_size("lat")
    scale = 1.0 / jnp.sqrt(jnp.float32(total_cells))
    weight_grad = kernel_sum.reshape(3, 3, chans, chans) * scale
    bias_grad = bias_sum[0] * scale
    return (outputs, input_grad, weight_grad, bias_grad)


def solution(mesh):
    in_specs = (P("lat", "lon", None), P(), P(), P("lat", "lon", None))
    out_specs = (P("lat", "lon", None), P("lat", "lon", None), P(), P())
    return jax.shard_map(shards, mesh=mesh, in_specs=in_specs, out_specs=out_specs, check_vma=False)
```

```python
import jax
import jax.numpy as jnp
from jax import lax
from jax.sharding import PartitionSpec as P


def extended(cells, sides, width, closed):
    for axis, dim in sides:
        count = lax.axis_size(axis)
        ends = count if closed else count - 1
        head = lax.slice_in_dim(cells, 0, width, axis=dim)
        tail = lax.slice_in_dim(cells, cells.shape[dim] - width, cells.shape[dim], axis=dim)
        cells = jnp.concatenate(
            [
                lax.ppermute(tail, axis, [(i, (i + 1) % count) for i in range(ends)]),
                cells,
                lax.ppermute(head, axis, [((i + 1) % count, i) for i in range(ends)]),
            ],
            axis=dim,
        )
    return cells


def from_behind(value, axis, steps):
    count = lax.axis_size(axis)
    pairs = [(source, (source + steps) % count) for source in range(count)]
    return lax.ppermute(value, axis, pairs)


def butterfly_sum(value, scatter, double):
    shape = value.shape
    data = value.reshape(-1)
    parts = 2 ** len(scatter)
    pad = (-data.shape[0]) % parts
    data = jnp.pad(data, (0, pad))
    history = []
    for axis, step in scatter:
        count = lax.axis_size(axis)
        bit = (lax.axis_index(axis) // step) % 2
        half = data.shape[0] // 2
        pairs = [(i, i ^ step) for i in range(count)]
        send = lax.dynamic_slice_in_dim(data, (1 - bit) * half, half)
        keep = lax.dynamic_slice_in_dim(data, bit * half, half)
        data = keep + lax.ppermute(send, axis, pairs)
        history.append((axis, step, bit))
    for axis, pairs in double:
        data = data + lax.ppermute(data, axis, pairs)
    for axis, step, bit in reversed(history):
        count = lax.axis_size(axis)
        pairs = [(i, i ^ step) for i in range(count)]
        other = lax.ppermute(data, axis, pairs)
        data = jnp.where(bit == 0, jnp.concatenate([data, other]), jnp.concatenate([other, data]))
    return data[: data.shape[0] - pad].reshape(shape)


def pairing_order(mesh_axes):
    near = []
    for axis in mesh_axes:
        step = 1
        while step < lax.axis_size(axis):
            near.append((axis, step))
            step *= 2
    ranked = [("lon", 1), ("lat", 1), ("lon", 4), ("lat", 2)]
    first = [pair for pair in ranked if pair in near]
    rest = [pair for pair in near if pair not in first]
    return first + rest


def reflected_ring_pairs(count, stride, size):
    pairs = []
    for i in range(count):
        z = (i // stride) % size
        if z % 2 == 0:
            w = (size - 2 - z) % size
        else:
            w = (size - z) % size
        pairs.append((i, i + (w - z) * stride))
    return pairs


def doubling_plan(rest):
    plan = []
    lon = lax.axis_size("lon")
    for axis, step in rest:
        count = lax.axis_size(axis)
        pairs = [(i, i ^ step) for i in range(count)]
        if axis == "lat" and step == 4 and count == 8:
            pairs = [(i, (3 - i // 2) * 2 + i % 2) for i in range(count)]
        if axis == "lon" and step == 16 and count == 32:
            pairs = reflected_ring_pairs(lon, 4, 8)
        plan.append((axis, pairs))
    return [step for step in plan if step[0] == "lat"] + [step for step in plan if step[0] != "lat"]


def shards(inputs, weight, bias, cotangent):
    rows, cols, chans = inputs.shape
    band = lax.axis_index("lat")
    bands = lax.axis_size("lat")
    half = lax.axis_size("lon") // 2
    both = jnp.concatenate([inputs, cotangent], axis=2)
    wide = extended(both, (("lon", 1),), 2, True)
    tall = extended(wide, (("lat", 0),), 2, False)
    far = from_behind(jnp.stack([wide[0], wide[-1]]), "lon", half)
    tall = tall.at[1].set(jnp.where(band == 0, far[0], tall[1]))
    tall = tall.at[rows + 2].set(jnp.where(band == bands - 1, far[1], tall[rows + 2]))
    padded = tall[:, :, :chans]
    ring_cot = tall[1:-1, 1:-1, chans:].astype(jnp.float32)
    pre = lax.conv_general_dilated(
        padded[None],
        weight,
        (1, 1),
        "VALID",
        dimension_numbers=("NHWC", "HWIO", "NHWC"),
        preferred_element_type=jnp.float32,
    )[0] + bias
    sig = jax.nn.sigmoid(pre)
    outputs = (pre * sig)[1:-1, 1:-1].astype(jnp.bfloat16)
    grad_ext = (ring_cot * sig * (1.0 + pre * (1.0 - sig))).astype(jnp.bfloat16)
    line = lax.broadcasted_iota(jnp.int32, (rows + 2, 1, 1), 0)
    outside = ((line == 0) & (band == 0)) | ((line == rows + 1) & (band == bands - 1))
    grad_ext = jnp.where(outside, jnp.zeros_like(grad_ext), grad_ext)
    pre_grad = grad_ext[1:-1, 1:-1].reshape(rows * cols, chans)
    flipped = jnp.transpose(weight[::-1, ::-1], (0, 1, 3, 2))
    cell_grad = lax.conv_general_dilated(
        grad_ext[None],
        flipped,
        (1, 1),
        "VALID",
        dimension_numbers=("NHWC", "HWIO", "NHWC"),
        preferred_element_type=jnp.float32,
    )[0]
    polar = []
    for line_at, tap_a in ((1, 0), (rows, 2)):
        ring = jnp.zeros((cols, chans), jnp.float32)
        for tap_b in range(3):
            ring = ring + jnp.dot(
                grad_ext[line_at, tap_b : tap_b + cols],
                weight[tap_a, 2 - tap_b].T,
                preferred_element_type=jnp.float32,
            )
        polar.append(ring)
    polar_in = from_behind(jnp.stack(polar).astype(jnp.bfloat16), "lon", half).astype(jnp.float32)
    cell_grad = cell_grad.at[0].add(jnp.where(band == 0, polar_in[0], 0.0))
    cell_grad = cell_grad.at[-1].add(jnp.where(band == bands - 1, polar_in[1], 0.0))
    input_grad = cell_grad.astype(jnp.bfloat16)
    taps = []
    for tap_a in range(3):
        for tap_b in range(3):
            window = padded[tap_a + 1 : tap_a + 1 + rows, tap_b + 1 : tap_b + 1 + cols].reshape(rows * cols, chans)
            taps.append(
                lax.dot_general(
                    window, pre_grad, (((0,), (0,)), ((), ())), preferred_element_type=jnp.float32
                )
            )
    kernel_terms = jnp.concatenate(taps, axis=0)
    bias_terms = jnp.sum(pre_grad.astype(jnp.float32), axis=0)[None, :]
    order = pairing_order(("lon", "lat"))
    sums = butterfly_sum(jnp.concatenate([kernel_terms, bias_terms], axis=0), order[:3], doubling_plan(order[3:]))
    kernel_sum, bias_sum = sums[:-1], sums[-1:]
    total_cells = rows * cols * lax.axis_size("lon") * lax.axis_size("lat")
    scale = 1.0 / jnp.sqrt(jnp.float32(total_cells))
    weight_grad = kernel_sum.reshape(3, 3, chans, chans) * scale
    bias_grad = bias_sum[0] * scale
    return (outputs, input_grad, weight_grad, bias_grad)


def solution(mesh):
    in_specs = (P("lat", "lon", None), P(), P(), P("lat", "lon", None))
    out_specs = (P("lat", "lon", None), P("lat", "lon", None), P(), P())
    return jax.shard_map(shards, mesh=mesh, in_specs=in_specs, out_specs=out_specs, check_vma=False)
```
